32 devices in a mesh: ep: 8 (over z, y), rep: 4 (over x, core).
Axes of the slice: x: 2, y: 2, z: 4, core: 2. Of those that a mesh axis runs over, the one named last changes fastest.
Arguments:
- residual: bfloat16 [4096, 2048], P(('rep', 'ep')), parts along dimension 0, may hold values from -6 to 6
- attn_out: bfloat16 [4096, 4096], P(('rep', 'ep')), parts along dimension 0, may hold values from -6 to 6
- out_weight: bfloat16 [4096, 2048], P('ep'), may hold values from -0.09375 to 0.09375
- post_gain: float32 [2048], replicated, may hold values from 0.1 to 1.9
- gate_up: bfloat16 [16, 2048, 1536], P('ep'), may hold values from -0.125 to 0.125
- down: bfloat16 [16, 768, 2048], P('ep'), may hold values from -0.21875 to 0.21875
- route_ids: int32 [4096, 8], P(('rep', 'ep')), parts along dimension 0, may hold values from 0 to 15, all different within a row; in each aligned block of 64 rows (0 to 63, 64 to 127, ...) at most 48 rows name the same one
- route_weight: float32 [4096, 8], P(('rep', 'ep')), parts along dimension 0, may hold values from 0.05 to 1
- final_gain: float32 [2048], replicated, may hold values from 0.1 to 1.9
Outputs:
- stream: bfloat16 [4096, 2048], P(('rep', 'ep')), parts along dimension 0
- next_input: bfloat16 [4096, 2048], P(('rep', 'ep')), parts along dimension 0
The draws below stay inside these ranges and needn't reach their ends.
There are 4 independent parts, one for each index of `rep`. The reference program is written for one: setup_inputs(seed, part) draws one part's arguments, and reference() takes and returns one part's arrays. A program takes and returns all parts, laid end to end along the dimension named above; an argument that names none is the same for every part. Nothing has to cross between parts.
Inputs may be any that keep to these rules, and one draw needn't show every extreme that they name: `route_ids`: each row names 8 different experts. In each aligned block of 64 rows of one device no expert is named by more than 48 rows, a bound that some block reaches.
All inputs are finite; a program needn't handle non-finite values.
Results may differ from the reference program's by a relative error of at most 0.014.
Values may be sent and summed in bfloat16 or wider, within the bound.
No kernel may reach another device: no remote copies, remote signals or barrier semaphores. Data moves between devices by JAX's collectives and lax.ppermute only.
A program may use at most 128 MiB of HBM per device.

```python
import math
import jax
import jax.numpy as jnp
import numpy as np
from jax import lax

D = 2048
FF = 768
ATT = 4096
TOP = 8
EXPERTS = 16
ROWS = 1024
BLOCK = 64
CAP = 48
N_EP = 8


def block_scale(rng, shape, cuts, low, largest):
    def one(dim, parts):
        heights = jax.random.uniform(jax.random.fold_in(jax.random.fold_in(rng, 6), dim), (parts,), jnp.float32, low / len(cuts), largest / len(cuts))
        return jnp.repeat(jnp.exp(heights), shape[dim] // parts).reshape((-1,) + (1,) * (len(shape) - dim - 1))

    gain = one(*cuts[0])
    for cut in cuts[1:]:
        gain = gain * one(*cut)
    return gain


def shared_out(own_key, own, number, rows, count, top, most, skew):
    sequence = jax.random.permutation(own_key, count)
    heavy_load, ordinary = load_shares(count, rows * top, most, skew, True), load_shares(count, rows * top, most, skew, False)
    places = jnp.arange(count)

    def named(sizes, turn):
        used = int((sizes > 0).sum())
        fixed = max(1, used // 4)
        moved = fixed + (places - fixed + turn * (used - fixed)) % max(1, count - fixed)
        return jnp.zeros((count,), jnp.int32).at[sequence[jnp.where(places < fixed, places, moved)]].set(jnp.asarray(sizes, jnp.int32))

    sizes = jnp.where(number % 4 == 0, named(heavy_load, number // 4), named(ordinary, number - number // 4 - 1))
    mixed = jax.random.permutation(jax.random.fold_in(own, 3), count)
    source_of, taker = mixed[0:count // 2 * 2:2], mixed[1:count // 2 * 2:2]
    margin = jnp.minimum(sizes[source_of] - 1, most - sizes[taker]) // 2
    margin = jnp.where((source_of == sequence[0]) | (taker == sequence[0]) | (sizes[taker] == 0), 0, jnp.maximum(margin, 0))
    moved = jax.random.randint(jax.random.fold_in(own, 4), (count // 2,), 0, 1 << 20) % (margin + 1)
    sizes = sizes.at[source_of].add(-moved).at[taker].add(moved)
    members = jnp.searchsorted(jnp.cumsum(sizes), jnp.arange(rows * top), side="right").astype(jnp.int32)
    listing = members.reshape(top, rows).T
    listing = listing[jax.random.permutation(jax.random.fold_in(own, 1), rows)]
    turn = jax.random.randint(jax.random.fold_in(own, 2), (rows, 1), 0, top)
    return jnp.take_along_axis(listing, (jnp.arange(top)[None, :] + turn) % top, axis=1)


def load_shares(amount, total, bound, lean, full):
    weights = [(1 << 20) // math.isqrt(grade ** lean) + 1 for grade in range(1, amount + 1)]
    largest = bound if full else min(bound, max(-(-total // amount), total * weights[0] // sum(weights)))
    least = 1 if total - largest >= amount - 1 else 0
    holding, rest = [largest] + [least] * (amount - 1), total - largest - least * (amount - 1)
    while rest > 0:
        free = [i for i in range(1, amount) if holding[i] < largest] or [i for i in range(1, amount) if holding[i] < bound]
        pool, remaining = sum([weights[i] for i in free]), rest
        for i in free:
            more = min(bound - holding[i], max(1, remaining * weights[i] // pool), rest)
            holding[i] = holding[i] + more
            rest = rest - more
    return np.array(holding)


def scatter_about(stream_key, shape, width, most, shards=(), held_as=jnp.bfloat16):
    result = width * jax.random.normal(stream_key, shape, jnp.float32)
    if shards:
        result = result * block_scale(stream_key, shape, shards, -0.22, 0.18)
    return jnp.clip(result, -most, most).astype(held_as)


def setup_inputs(seed: int = 0, part: int = 0) -> dict:
    key_of = jax.random.split(jax.random.key(seed), 10)
    own_keys = jax.random.split(jax.random.fold_in(key_of[9], part), 10)
    residual = scatter_about(own_keys[0], (ROWS, D), 1.0, 6.0, ((0, 8),))
    attn_out = scatter_about(own_keys[1], (ROWS, ATT), 1.0, 6.0, ((0, 8),))
    out_weight = scatter_about(key_of[2], (ATT, D), ATT ** -0.5, 0.09375, ((0, 8),))
    post_gain = jnp.clip(1.0 + 0.18 * jax.random.normal(key_of[3], (D,), jnp.float32), 0.1, 1.9)
    gate_up = scatter_about(key_of[4], (EXPERTS, D, 2 * FF), D ** -0.5, 0.125, ((0, 8),))
    down = scatter_about(key_of[5], (EXPERTS, FF, D), FF ** -0.5, 0.21875, ((0, 8),))
    route_ids_keys = jax.random.split(jax.random.fold_in(own_keys[6], 1), ROWS // BLOCK)
    route_ids_turns = jax.random.permutation(jax.random.fold_in(own_keys[6], 3), ROWS // BLOCK)
    route_ids = jax.vmap(lambda own, number: shared_out(jax.random.fold_in(own_keys[6], 2), own, number, BLOCK, EXPERTS, TOP, CAP, 2))(route_ids_keys, route_ids_turns).reshape((ROWS, TOP))
    route_weight = jnp.clip(jnp.exp(math.log(1.0) - 2.9957323 * jax.random.uniform(own_keys[7], (ROWS, TOP), jnp.float32) ** block_scale(own_keys[7], (ROWS, TOP), ((0, 8),), -0.2, 0.2)), 0.05, 1.0)
    final_gain = jnp.clip(1.0 + 0.18 * jax.random.normal(key_of[8], (D,), jnp.float32), 0.1, 1.9)
    return {"residual": residual, "attn_out": attn_out, "out_weight": out_weight, "post_gain": post_gain, "gate_up": gate_up, "down": down, "route_ids": route_ids, "route_weight": route_weight, "final_gain": final_gain}


def rms_scale(values, scale_gain):
    mean_square = lax.optimization_barrier(jnp.mean(values * values, axis=-1, keepdims=True))
    return values * lax.rsqrt(mean_square + 1e-06) * scale_gain

def expert_rows(inputs, weights_in, weights_out):
    hidden_width = weights_out.shape[0]
    projected = jnp.dot(inputs, weights_in, preferred_element_type=jnp.float32)
    activated = (jax.nn.silu(projected[:, :hidden_width]) * projected[:, hidden_width:]).astype(jnp.bfloat16)
    return jnp.dot(activated, weights_out, preferred_element_type=jnp.float32).astype(jnp.bfloat16)

def apply_expert(bundle):
    return expert_rows(bundle[0], bundle[1], bundle[2])

def reference(residual, attn_out, out_weight, post_gain, gate_up, down, route_ids, route_weight, final_gain):
    row_count = residual.shape[0]
    experts = gate_up.shape[0]
    top_count = route_ids.shape[1]
    projected = jnp.dot(attn_out, out_weight, preferred_element_type=jnp.float32)
    middle = (residual.astype(jnp.float32) + projected).astype(jnp.bfloat16)
    normed = rms_scale(middle.astype(jnp.float32), post_gain).astype(jnp.bfloat16)
    blocks = row_count // BLOCK
    slot_count = 2 * CAP * N_EP
    targets = route_ids.reshape(blocks, BLOCK * top_count)
    onehot = (targets[:, :, None] == jnp.arange(experts, dtype=jnp.int32)).astype(jnp.int32)
    slot_rank = lax.optimization_barrier(jnp.sum(jnp.cumsum(onehot, axis=1) * onehot, axis=2)) - 1
    block_index = jnp.arange(blocks, dtype=jnp.int32)[:, None]
    position = block_index // 2 * (2 * CAP) + block_index % 2 * CAP + slot_rank
    flat_index = (targets * slot_count + position).reshape(-1).astype(jnp.int32)
    source = jnp.repeat(normed, top_count, axis=0)
    buffer = jnp.zeros((experts * slot_count, D), jnp.bfloat16).at[flat_index].set(source)
    outputs = lax.map(apply_expert, (buffer.reshape(experts, slot_count, D), gate_up, down))
    picked = outputs.reshape(experts * slot_count, D)[flat_index].reshape(row_count, top_count, D)
    combined = lax.optimization_barrier(jnp.sum(picked.astype(jnp.float32) * route_weight[:, :, None], axis=1))
    updated = middle.astype(jnp.float32) + combined
    return (updated.astype(jnp.bfloat16), rms_scale(updated, final_gain).astype(jnp.bfloat16))
```

```python
import jax
import jax.numpy as jnp
from jax import lax
from jax.sharding import PartitionSpec as P


def rms_scale(values, scale_gain):
    mean_square = jnp.mean(values * values, axis=-1, keepdims=True)
    return values * lax.rsqrt(mean_square + 1e-06) * scale_gain


def body(
    residual, attn_out, out_weight, post_gain, gate_up, down, route_ids, route_weight, final_gain
):
    row_count, model_width = residual.shape
    ep_size = lax.axis_size("ep")
    me = lax.axis_index("ep")
    local_experts = gate_up.shape[0]
    hidden_width = down.shape[1]
    slice_width = out_weight.shape[0]
    group_rows = row_count * ep_size

    with jax.named_scope("out_projection"):
        columns = attn_out.reshape(row_count, ep_size, slice_width).transpose(1, 0, 2)
        columns = lax.all_to_all(columns, "ep", split_axis=0, concat_axis=0, tiled=True)
        partial = jnp.dot(
            columns.reshape(group_rows, slice_width), out_weight, preferred_element_type=jnp.float32
        )
        owner = (lax.broadcasted_iota(jnp.int32, (group_rows, 1), 0) // row_count) == me
        padded_residual = jnp.tile(residual.astype(jnp.float32), (ep_size, 1))
        partial = partial + jnp.where(owner, padded_residual, 0.0)
        middle_all = lax.psum(partial.astype(jnp.bfloat16), "ep")

    normed_all = rms_scale(middle_all.astype(jnp.float32), post_gain).astype(jnp.bfloat16)
    ids_all = lax.all_gather(route_ids, "ep", axis=0, tiled=True)
    weights_all = lax.all_gather(route_weight, "ep", axis=0, tiled=True)

    with jax.named_scope("local_experts"):
        combined_part = jnp.zeros((group_rows, model_width), jnp.float32)
        for e in range(local_experts):
            expert_id = me * local_experts + e
            row_weight = jnp.sum(jnp.where(ids_all == expert_id, weights_all, 0.0), axis=1)
            projected_up = jnp.dot(normed_all, gate_up[e], preferred_element_type=jnp.float32)
            activated = (
                jax.nn.silu(projected_up[:, :hidden_width]) * projected_up[:, hidden_width:]
            ).astype(jnp.bfloat16)
            expert_out = jnp.dot(activated, down[e], preferred_element_type=jnp.float32).astype(
                jnp.bfloat16
            )
            combined_part = combined_part + row_weight[:, None] * expert_out.astype(jnp.float32)

    with jax.named_scope("combine_return"):
        combined = lax.psum_scatter(
            combined_part.astype(jnp.bfloat16), "ep", scatter_dimension=0, tiled=True
        )
    middle = lax.dynamic_slice_in_dim(middle_all, me * row_count, row_count, axis=0)
    updated = middle.astype(jnp.float32) + combined.astype(jnp.float32)
    return (updated.astype(jnp.bfloat16), rms_scale(updated, final_gain).astype(jnp.bfloat16))


def solution(mesh):
    in_specs = (
        P(("rep", "ep"), None),
        P(("rep", "ep"), None),
        P("ep", None),
        P(),
        P("ep", None, None),
        P("ep", None, None),
        P(("rep", "ep"), None),
        P(("rep", "ep"), None),
        P(),
    )
    out_specs = (P(("rep", "ep"), None), P(("rep", "ep"), None))
    return jax.shard_map(body, mesh=mesh, in_specs=in_specs, out_specs=out_specs, check_vma=False)
```

```python
import jax
import jax.numpy as jnp
from jax import lax
from jax.sharding import PartitionSpec as P


def rms_scale(values, scale_gain):
    mean_square = jnp.mean(values * values, axis=-1, keepdims=True)
    return values * lax.rsqrt(mean_square + 1e-06) * scale_gain


def body(
    residual, attn_out, out_weight, post_gain, gate_up, down, route_ids, route_weight, final_gain
):
    row_count, model_width = residual.shape
    ep_size = lax.axis_size("ep")
    me = lax.axis_index("ep")
    local_experts = gate_up.shape[0]
    hidden_width = down.shape[1]
    slice_width = out_weight.shape[0]
    group_rows = row_count * ep_size

    with jax.named_scope("route_weights"):
        expert_ids = jnp.arange(local_experts * ep_size, dtype=jnp.int32)
        dense_weight = jnp.sum(
            jnp.where(route_ids[:, :, None] == expert_ids, route_weight[:, :, None], 0.0), axis=1
        )
        dense_weight = dense_weight.reshape(row_count, ep_size, local_experts).transpose(1, 0, 2)
        row_weights = lax.all_to_all(dense_weight, "ep", split_axis=0, concat_axis=0, tiled=True)
        row_weights = row_weights.reshape(group_rows, local_experts)

    with jax.named_scope("out_projection"):
        columns = attn_out.reshape(row_count, ep_size, slice_width).transpose(1, 0, 2)
        columns = lax.all_to_all(columns, "ep", split_axis=0, concat_axis=0, tiled=True)
        partial = jnp.dot(
            columns.reshape(group_rows, slice_width), out_weight, preferred_element_type=jnp.float32
        )
        owner = (lax.broadcasted_iota(jnp.int32, (group_rows, 1), 0) // row_count) == me
        padded_residual = jnp.tile(residual.astype(jnp.float32), (ep_size, 1))
        partial = partial + jnp.where(owner, padded_residual, 0.0)
        middle_all = lax.psum(partial.astype(jnp.bfloat16), "ep")

    normed_all = rms_scale(middle_all.astype(jnp.float32), post_gain).astype(jnp.bfloat16)
    with jax.named_scope("local_experts"):
        combined_part = jnp.zeros((group_rows, model_width), jnp.float32)
        for e in range(local_experts):
            row_weight = row_weights[:, e]
            projected_up = jnp.dot(normed_all, gate_up[e], preferred_element_type=jnp.float32)
            activated = (
                jax.nn.silu(projected_up[:, :hidden_width]) * projected_up[:, hidden_width:]
            ).astype(jnp.bfloat16)
            expert_out = jnp.dot(activated, down[e], preferred_element_type=jnp.float32).astype(
                jnp.bfloat16
            )
            combined_part = combined_part + row_weight[:, None] * expert_out.astype(jnp.float32)

    with jax.named_scope("combine_return"):
        combined = lax.psum_scatter(
            combined_part.astype(jnp.bfloat16), "ep", scatter_dimension=0, tiled=True
        )
    middle = lax.dynamic_slice_in_dim(middle_all, me * row_count, row_count, axis=0)
    updated = middle.astype(jnp.float32) + combined.astype(jnp.float32)
    return (updated.astype(jnp.bfloat16), rms_scale(updated, final_gain).astype(jnp.bfloat16))


def solution(mesh):
    in_specs = (
        P(("rep", "ep"), None),
        P(("rep", "ep"), None),
        P("ep", None),
        P(),
        P("ep", None, None),
        P("ep", None, None),
        P(("rep", "ep"), None),
        P(("rep", "ep"), None),
        P(),
    )
    out_specs = (P(("rep", "ep"), None), P(("rep", "ep"), None))
    return jax.shard_map(body, mesh=mesh, in_specs=in_specs, out_specs=out_specs, check_vma=False)
```

```python
import jax
import jax.numpy as jnp
from jax import lax
from jax.sharding import PartitionSpec as P


def rms_scale(values, scale_gain):
    mean_square = jnp.mean(values * values, axis=-1, keepdims=True)
    return values * lax.rsqrt(mean_square + 1e-06) * scale_gain


def ring_order(n):
    if n % 2:
        return list(range(n))
    return list(range(0, n, 2)) + list(range(n - 1, 0, -2))


def ring_reduce_scatter(blocks, ring, pos):
    n, rows, _ = blocks.shape
    half = rows // 2
    ring_index = jnp.array(ring, dtype=jnp.int32)
    forward = [(ring[q], ring[(q + 1) % n]) for q in range(n)]
    backward = [(ring[q], ring[(q - 1) % n]) for q in range(n)]
    got_fwd = got_bwd = None
    for step in range(n - 1):
        owner_fwd = ring_index[(pos - 1 - step) % n]
        owner_bwd = ring_index[(pos + 1 + step) % n]
        send_fwd = lax.dynamic_index_in_dim(blocks, owner_fwd, 0, keepdims=False)[:half]
        send_bwd = lax.dynamic_index_in_dim(blocks, owner_bwd, 0, keepdims=False)[half:]
        if step:
            send_fwd = send_fwd + got_fwd
            send_bwd = send_bwd + got_bwd
        got_fwd = lax.ppermute(send_fwd.astype(jnp.bfloat16), "ep", forward).astype(jnp.float32)
        got_bwd = lax.ppermute(send_bwd.astype(jnp.bfloat16), "ep", backward).astype(jnp.float32)
    me = ring_index[pos]
    own = lax.dynamic_index_in_dim(blocks, me, 0, keepdims=False)
    return jnp.concatenate([own[:half] + got_fwd, own[half:] + got_bwd], axis=0)


def ring_all_gather(block, ring, pos):
    n = len(ring)
    rows = block.shape[0]
    half = rows // 2
    ring_index = jnp.array(ring, dtype=jnp.int32)
    forward = [(ring[q], ring[(q + 1) % n]) for q in range(n)]
    backward = [(ring[q], ring[(q - 1) % n]) for q in range(n)]
    out = jnp.zeros((n,) + block.shape, block.dtype)
    out = lax.dynamic_update_index_in_dim(out, block, ring_index[pos], 0)
    got_fwd, got_bwd = block[:half], block[half:]
    for step in range(n - 1):
        got_fwd = lax.ppermute(got_fwd, "ep", forward)
        got_bwd = lax.ppermute(got_bwd, "ep", backward)
        src_fwd = ring_index[(pos - 1 - step) % n]
        src_bwd = ring_index[(pos + 1 + step) % n]
        out = lax.dynamic_update_slice(out, got_fwd[None], (src_fwd, 0, 0))
        out = lax.dynamic_update_slice(out, got_bwd[None], (src_bwd, half, 0))
    return out


def body(
    residual, attn_out, out_weight, post_gain, gate_up, down, route_ids, route_weight, final_gain
):
    row_count, model_width = residual.shape
    ep_size = lax.axis_size("ep")
    me = lax.axis_index("ep")
    local_experts = gate_up.shape[0]
    hidden_width = down.shape[1]
    slice_width = out_weight.shape[0]
    group_rows = row_count * ep_size
    ring = ring_order(ep_size)
    pos = jnp.array([ring.index(p) for p in range(ep_size)], dtype=jnp.int32)[me]

    with jax.named_scope("route_weights"):
        expert_ids = jnp.arange(local_experts * ep_size, dtype=jnp.int32)
        dense_weight = jnp.sum(
            jnp.where(route_ids[:, :, None] == expert_ids, route_weight[:, :, None], 0.0), axis=1
        )
        dense_weight = dense_weight.reshape(row_count, ep_size, local_experts).transpose(1, 0, 2)
        row_weights = lax.all_to_all(dense_weight, "ep", split_axis=0, concat_axis=0, tiled=True)
        row_weights = row_weights.reshape(group_rows, local_experts)

    with jax.named_scope("out_projection"):
        columns = attn_out.reshape(row_count, ep_size, slice_width).transpose(1, 0, 2)
        columns = lax.all_to_all(columns, "ep", split_axis=0, concat_axis=0, tiled=True)
        partial = jnp.dot(
            columns.reshape(group_rows, slice_width), out_weight, preferred_element_type=jnp.float32
        )
        projected = ring_reduce_scatter(partial.reshape(ep_size, row_count, model_width), ring, pos)
        middle = (residual.astype(jnp.float32) + projected).astype(jnp.bfloat16)

    normed = rms_scale(middle.astype(jnp.float32), post_gain).astype(jnp.bfloat16)
    with jax.named_scope("dispatch_gather"):
        normed_all = ring_all_gather(normed, ring, pos).reshape(group_rows, model_width)

    with jax.named_scope("local_experts"):
        combined_part = jnp.zeros((group_rows, model_width), jnp.float32)
        for e in range(local_experts):
            row_weight = row_weights[:, e]
            projected_up = jnp.dot(normed_all, gate_up[e], preferred_element_type=jnp.float32)
            activated = (
                jax.nn.silu(projected_up[:, :hidden_width]) * projected_up[:, hidden_width:]
            ).astype(jnp.bfloat16)
            expert_out = jnp.dot(activated, down[e], preferred_element_type=jnp.float32).astype(
                jnp.bfloat16
            )
            combined_part = combined_part + row_weight[:, None] * expert_out.astype(jnp.float32)

    with jax.named_scope("combine_return"):
        combined = ring_reduce_scatter(
            combined_part.reshape(ep_size, row_count, model_width), ring, pos
        )
    updated = middle.astype(jnp.float32) + combined
    return (updated.astype(jnp.bfloat16), rms_scale(updated, final_gain).astype(jnp.bfloat16))


def solution(mesh):
    in_specs = (
        P(("rep", "ep"), None),
        P(("rep", "ep"), None),
        P("ep", None),
        P(),
        P("ep", None, None),
        P("ep", None, None),
        P(("rep", "ep"), None),
        P(("rep", "ep"), None),
        P(),
    )
    out_specs = (P(("rep", "ep"), None), P(("rep", "ep"), None))
    return jax.shard_map(body, mesh=mesh, in_specs=in_specs, out_specs=out_specs, check_vma=False)
```

```python
import jax
import jax.numpy as jnp
from jax import lax
from jax.sharding import PartitionSpec as P


def rms_scale(values, scale_gain):
    mean_square = jnp.mean(values * values, axis=-1, keepdims=True)
    return values * lax.rsqrt(mean_square + 1e-06) * scale_gain


def ring_order(n):
    if n % 2:
        return list(range(n))
    return list(range(0, n, 2)) + list(range(n - 1, 0, -2))


def ring_reduce_scatter(blocks, ring, pos):
    n, rows, _ = blocks.shape
    half = rows // 2
    ring_index = jnp.array(ring, dtype=jnp.int32)
    forward = [(ring[q], ring[(q + 1) % n]) for q in range(n)]
    backward = [(ring[q], ring[(q - 1) % n]) for q in range(n)]
    got_fwd = got_bwd = None
    for step in range(n - 1):
        owner_fwd = ring_index[(pos - 1 - step) % n]
        owner_bwd = ring_index[(pos + 1 + step) % n]
        send_fwd = lax.dynamic_index_in_dim(blocks, owner_fwd, 0, keepdims=False)[:half]
        send_bwd = lax.dynamic_index_in_dim(blocks, owner_bwd, 0, keepdims=False)[half:]
        if step:
            send_fwd = send_fwd + got_fwd
            send_bwd = send_bwd + got_bwd
        send_fwd, send_bwd = lax.optimization_barrier(
            (send_fwd.astype(jnp.bfloat16), send_bwd.astype(jnp.bfloat16))
        )
        got_fwd, got_bwd = lax.optimization_barrier(
            (lax.ppermute(send_fwd, "ep", forward), lax.ppermute(send_bwd, "ep", backward))
        )
        got_fwd = got_fwd.astype(jnp.float32)
        got_bwd = got_bwd.astype(jnp.float32)
    me = ring_index[pos]
    own = lax.dynamic_index_in_dim(blocks, me, 0, keepdims=False)
    return jnp.concatenate([own[:half] + got_fwd, own[half:] + got_bwd], axis=0)


def ring_all_gather(block, ring, pos):
    n = len(ring)
    rows = block.shape[0]
    half = rows // 2
    ring_index = jnp.array(ring, dtype=jnp.int32)
    forward = [(ring[q], ring[(q + 1) % n]) for q in range(n)]
    backward = [(ring[q], ring[(q - 1) % n]) for q in range(n)]
    out = jnp.zeros((n,) + block.shape, block.dtype)
    out = lax.dynamic_update_index_in_dim(out, block, ring_index[pos], 0)
    got_fwd, got_bwd = block[:half], block[half:]
    for step in range(n - 1):
        got_fwd, got_bwd = lax.optimization_barrier(
            (lax.ppermute(got_fwd, "ep", forward), lax.ppermute(got_bwd, "ep", backward))
        )
        src_fwd = ring_index[(pos - 1 - step) % n]
        src_bwd = ring_index[(pos + 1 + step) % n]
        out = lax.dynamic_update_slice(out, got_fwd[None], (src_fwd, 0, 0))
        out = lax.dynamic_update_slice(out, got_bwd[None], (src_bwd, half, 0))
    return out


def body(
    residual, attn_out, out_weight, post_gain, gate_up, down, route_ids, route_weight, final_gain
):
    row_count, model_width = residual.shape
    ep_size = lax.axis_size("ep")
    me = lax.axis_index("ep")
    local_experts = gate_up.shape[0]
    hidden_width = down.shape[1]
    slice_width = out_weight.shape[0]
    group_rows = row_count * ep_size
    ring = ring_order(ep_size)
    pos = jnp.array([ring.index(p) for p in range(ep_size)], dtype=jnp.int32)[me]

    with jax.named_scope("route_weights"):
        expert_ids = jnp.arange(local_experts * ep_size, dtype=jnp.int32)
        dense_weight = jnp.sum(
            jnp.where(route_ids[:, :, None] == expert_ids, route_weight[:, :, None], 0.0), axis=1
        )
        dense_weight = dense_weight.reshape(row_count, ep_size, local_experts).transpose(1, 0, 2)
        row_weights = lax.all_to_all(dense_weight, "ep", split_axis=0, concat_axis=0, tiled=True)
        row_weights = row_weights.reshape(group_rows, local_experts)

    with jax.named_scope("out_projection"):
        columns = attn_out.reshape(row_count, ep_size, slice_width).transpose(1, 0, 2)
        columns = lax.all_to_all(columns, "ep", split_axis=0, concat_axis=0, tiled=True)
        columns, row_weights = lax.optimization_barrier((columns, row_weights))
        partial = jnp.dot(
            columns.reshape(group_rows, slice_width), out_weight, preferred_element_type=jnp.float32
        )
        projected = ring_reduce_scatter(partial.reshape(ep_size, row_count, model_width), ring, pos)
        middle = (residual.astype(jnp.float32) + projected).astype(jnp.bfloat16)

    normed = rms_scale(middle.astype(jnp.float32), post_gain).astype(jnp.bfloat16)
    with jax.named_scope("dispatch_gather"):
        normed_all = ring_all_gather(normed, ring, pos).reshape(group_rows, model_width)

    with jax.named_scope("local_experts"):
        combined_part = jnp.zeros((group_rows, model_width), jnp.float32)
        for e in range(local_experts):
            row_weight = row_weights[:, e]
            projected_up = jnp.dot(normed_all, gate_up[e], preferred_element_type=jnp.float32)
            activated = (
                jax.nn.silu(projected_up[:, :hidden_width]) * projected_up[:, hidden_width:]
            ).astype(jnp.bfloat16)
            expert_out = jnp.dot(activated, down[e], preferred_element_type=jnp.float32).astype(
                jnp.bfloat16
            )
            combined_part = combined_part + row_weight[:, None] * expert_out.astype(jnp.float32)

    with jax.named_scope("combine_return"):
        combined = ring_reduce_scatter(
            combined_part.reshape(ep_size, row_count, model_width), ring, pos
        )
    updated = middle.astype(jnp.float32) + combined
    return (updated.astype(jnp.bfloat16), rms_scale(updated, final_gain).astype(jnp.bfloat16))


def solution(mesh):
    in_specs = (
        P(("rep", "ep"), None),
        P(("rep", "ep"), None),
        P("ep", None),
        P(),
        P("ep", None, None),
        P("ep", None, None),
        P(("rep", "ep"), None),
        P(("rep", "ep"), None),
        P(),
    )
    out_specs = (P(("rep", "ep"), None), P(("rep", "ep"), None))
    return jax.shard_map(body, mesh=mesh, in_specs=in_specs, out_specs=out_specs, check_vma=False)
```

```python
import jax
import jax.numpy as jnp
from jax import lax
from jax.sharding import PartitionSpec as P


def rms_scale(values, scale_gain):
    mean_square = jnp.mean(values * values, axis=-1, keepdims=True)
    return values * lax.rsqrt(mean_square + 1e-06) * scale_gain


def ring_order(n):
    if n % 2:
        return list(range(n))
    return list(range(0, n, 2)) + list(range(n - 1, 0, -2))


def ring_reduce_scatter(blocks, ring, pos):
    n, rows, _ = blocks.shape
    half = rows // 2
    ring_index = jnp.array(ring, dtype=jnp.int32)
    forward = [(ring[q], ring[(q + 1) % n]) for q in range(n)]
    backward = [(ring[q], ring[(q - 1) % n]) for q in range(n)]
    got_fwd = got_bwd = None
    for step in range(n - 1):
        owner_fwd = ring_index[(pos - 1 - step) % n]
        owner_bwd = ring_index[(pos + 1 + step) % n]
        send_fwd = lax.dynamic_index_in_dim(blocks, owner_fwd, 0, keepdims=False)[:half]
        send_bwd = lax.dynamic_index_in_dim(blocks, owner_bwd, 0, keepdims=False)[half:]
        if step:
            send_fwd = send_fwd + got_fwd
            send_bwd = send_bwd + got_bwd
        send_fwd, send_bwd = lax.optimization_barrier(
            (send_fwd.astype(jnp.bfloat16), send_bwd.astype(jnp.bfloat16))
        )
        got_fwd, got_bwd = lax.optimization_barrier(
            (lax.ppermute(send_fwd, "ep", forward), lax.ppermute(send_bwd, "ep", backward))
        )
        got_fwd = got_fwd.astype(jnp.float32)
        got_bwd = got_bwd.astype(jnp.float32)
    me = ring_index[pos]
    own = lax.dynamic_index_in_dim(blocks, me, 0, keepdims=False)
    return jnp.concatenate([own[:half] + got_fwd, own[half:] + got_bwd], axis=0)


def ring_all_gather(block, ring, pos):
    n = len(ring)
    half = block.shape[0] // 2
    forward = [(ring[q], ring[(q + 1) % n]) for q in range(n)]
    backward = [(ring[q], ring[(q - 1) % n]) for q in range(n)]
    got_fwd, got_bwd = block[:half], block[half:]
    arrived = []
    for step in range(n - 1):
        got_fwd, got_bwd = lax.optimization_barrier(
            (lax.ppermute(got_fwd, "ep", forward), lax.ppermute(got_bwd, "ep", backward))
        )
        arrived.append((got_fwd, got_bwd))
    return arrived


def ring_reduce_scatter_steps(pieces, own, ring):
    n = len(ring)
    forward = [(ring[q], ring[(q + 1) % n]) for q in range(n)]
    backward = [(ring[q], ring[(q - 1) % n]) for q in range(n)]
    got_fwd = got_bwd = None
    for step in range(n - 1):
        send_fwd, send_bwd = pieces[step]
        if step:
            send_fwd = send_fwd + got_fwd
            send_bwd = send_bwd + got_bwd
        send_fwd, send_bwd = lax.optimization_barrier(
            (send_fwd.astype(jnp.bfloat16), send_bwd.astype(jnp.bfloat16))
        )
        got_fwd, got_bwd = lax.optimization_barrier(
            (lax.ppermute(send_fwd, "ep", forward), lax.ppermute(send_bwd, "ep", backward))
        )
        got_fwd = got_fwd.astype(jnp.float32)
        got_bwd = got_bwd.astype(jnp.float32)
    half = own.shape[0] // 2
    return jnp.concatenate([own[:half] + got_fwd, own[half:] + got_bwd], axis=0)


def expert_mix(rows, weights, gate_up, down):
    hidden_width = down.shape[1]
    total = None
    for e in range(gate_up.shape[0]):
        projected_up = jnp.dot(rows, gate_up[e], preferred_element_type=jnp.float32)
        activated = (
            jax.nn.silu(projected_up[:, :hidden_width]) * projected_up[:, hidden_width:]
        ).astype(jnp.bfloat16)
        expert_out = jnp.dot(activated, down[e], preferred_element_type=jnp.float32).astype(
            jnp.bfloat16
        )
        term = weights[:, e : e + 1] * expert_out.astype(jnp.float32)
        total = term if total is None else total + term
    return total


def body(
    residual, attn_out, out_weight, post_gain, gate_up, down, route_ids, route_weight, final_gain
):
    row_count, model_width = residual.shape
    ep_size = lax.axis_size("ep")
    me = lax.axis_index("ep")
    local_experts = gate_up.shape[0]
    hidden_width = down.shape[1]
    slice_width = out_weight.shape[0]
    group_rows = row_count * ep_size
    ring = ring_order(ep_size)
    pos = jnp.array([ring.index(p) for p in range(ep_size)], dtype=jnp.int32)[me]

    with jax.named_scope("route_weights"):
        expert_ids = jnp.arange(local_experts * ep_size, dtype=jnp.int32)
        dense_weight = jnp.sum(
            jnp.where(route_ids[:, :, None] == expert_ids, route_weight[:, :, None], 0.0), axis=1
        )
        dense_weight = dense_weight.reshape(row_count, ep_size, local_experts).transpose(1, 0, 2)
        row_weights = lax.all_to_all(dense_weight, "ep", split_axis=0, concat_axis=0, tiled=True)
        row_weights = row_weights.reshape(group_rows, local_experts)

    with jax.named_scope("out_projection"):
        columns = attn_out.reshape(row_count, ep_size, slice_width).transpose(1, 0, 2)
        columns = lax.all_to_all(columns, "ep", split_axis=0, concat_axis=0, tiled=True)
        columns, row_weights = lax.optimization_barrier((columns, row_weights))
        partial = jnp.dot(
            columns.reshape(group_rows, slice_width), out_weight, preferred_element_type=jnp.float32
        )
        projected = ring_reduce_scatter(partial.reshape(ep_size, row_count, model_width), ring, pos)
        middle = (residual.astype(jnp.float32) + projected).astype(jnp.bfloat16)

    normed = rms_scale(middle.astype(jnp.float32), post_gain).astype(jnp.bfloat16)
    with jax.named_scope("dispatch_gather"):
        arrived = ring_all_gather(normed, ring, pos)

    ring_index = jnp.array(ring, dtype=jnp.int32)
    weight_blocks = row_weights.reshape(ep_size, row_count, local_experts)
    half = row_count // 2

    def step_weights(step):
        owner_fwd = ring_index[(pos - 1 - step) % ep_size]
        owner_bwd = ring_index[(pos + 1 + step) % ep_size]
        w_fwd = lax.dynamic_index_in_dim(weight_blocks, owner_fwd, 0, keepdims=False)[:half]
        w_bwd = lax.dynamic_index_in_dim(weight_blocks, owner_bwd, 0, keepdims=False)[half:]
        return w_fwd, w_bwd

    with jax.named_scope("local_experts"):
        first = (ep_size - 1 + 1) // 2
        chunks = [list(range(first)), list(range(first, ep_size - 1))]
        pieces = [None] * (ep_size - 1)
        own_part = None
        for c, steps in enumerate(chunks):
            rows_in = []
            weights_in = []
            for step in steps:
                rows_in += list(arrived[step])
                weights_in += list(step_weights(step))
            if c == len(chunks) - 1:
                rows_in.append(normed)
                weights_in.append(lax.dynamic_index_in_dim(weight_blocks, me, 0, keepdims=False))
            mixed = expert_mix(
                jnp.concatenate(rows_in, axis=0), jnp.concatenate(weights_in, axis=0), gate_up, down
            )
            for i, step in enumerate(steps):
                pieces[step] = (mixed[(2 * i) * half : (2 * i + 1) * half],
                                mixed[(2 * i + 1) * half : (2 * i + 2) * half])
            if c == len(chunks) - 1:
                own_part = mixed[2 * len(steps) * half :]

    with jax.named_scope("combine_return"):
        combined = ring_reduce_scatter_steps(pieces, own_part, ring)
    updated = middle.astype(jnp.float32) + combined
    return (updated.astype(jnp.bfloat16), rms_scale(updated, final_gain).astype(jnp.bfloat16))


def solution(mesh):
    in_specs = (
        P(("rep", "ep"), None),
        P(("rep", "ep"), None),
        P("ep", None),
        P(),
        P("ep", None, None),
        P("ep", None, None),
        P(("rep", "ep"), None),
        P(("rep", "ep"), None),
        P(),
    )
    out_specs = (P(("rep", "ep"), None), P(("rep", "ep"), None))
    return jax.shard_map(body, mesh=mesh, in_specs=in_specs, out_specs=out_specs, check_vma=False)
```

```python
import jax
import jax.numpy as jnp
from jax import lax
from jax.sharding import PartitionSpec as P


def rms_scale(values, scale_gain):
    mean_square = jnp.mean(values * values, axis=-1, keepdims=True)
    return values * lax.rsqrt(mean_square + 1e-06) * scale_gain


def ring_order(n):
    if n % 2:
        return list(range(n))
    return list(range(0, n, 2)) + list(range(n - 1, 0, -2))


def ring_all_gather(block, ring, pos):
    n = len(ring)
    half = block.shape[0] // 2
    forward = [(ring[q], ring[(q + 1) % n]) for q in range(n)]
    backward = [(ring[q], ring[(q - 1) % n]) for q in range(n)]
    got_fwd, got_bwd = block[:half], block[half:]
    arrived = []
    for step in range(n - 1):
        got_fwd, got_bwd = lax.optimization_barrier(
            (lax.ppermute(got_fwd, "ep", forward), lax.ppermute(got_bwd, "ep", backward))
        )
        arrived.append((got_fwd, got_bwd))
    return arrived


def ring_reduce_scatter_steps(pieces, own, ring):
    n = len(ring)
    forward = [(ring[q], ring[(q + 1) % n]) for q in range(n)]
    backward = [(ring[q], ring[(q - 1) % n]) for q in range(n)]
    got_fwd = got_bwd = None
    for step in range(n - 1):
        send_fwd, send_bwd = pieces[step]
        if step:
            send_fwd = send_fwd + got_fwd
            send_bwd = send_bwd + got_bwd
        send_fwd, send_bwd = lax.optimization_barrier(
            (send_fwd.astype(jnp.bfloat16), send_bwd.astype(jnp.bfloat16))
        )
        got_fwd, got_bwd = lax.optimization_barrier(
            (lax.ppermute(send_fwd, "ep", forward), lax.ppermute(send_bwd, "ep", backward))
        )
        got_fwd = got_fwd.astype(jnp.float32)
        got_bwd = got_bwd.astype(jnp.float32)
    half = own.shape[0] // 2
    return jnp.concatenate([own[:half] + got_fwd, own[half:] + got_bwd], axis=0)


def expert_mix(rows, weights, gate_up, down):
    hidden_width = down.shape[1]
    total = None
    for e in range(gate_up.shape[0]):
        projected_up = jnp.dot(rows, gate_up[e], preferred_element_type=jnp.float32)
        activated = (
            jax.nn.silu(projected_up[:, :hidden_width]) * projected_up[:, hidden_width:]
        ).astype(jnp.bfloat16)
        expert_out = jnp.dot(activated, down[e], preferred_element_type=jnp.float32).astype(
            jnp.bfloat16
        )
        term = weights[:, e : e + 1] * expert_out.astype(jnp.float32)
        total = term if total is None else total + term
    return total


def split_exact(values):
    first = lax.reduce_precision(values, exponent_bits=8, mantissa_bits=7)
    rest = values - first
    second = lax.reduce_precision(rest, exponent_bits=8, mantissa_bits=7)
    third = rest - second
    return jnp.concatenate([first, second, third], axis=-1).astype(jnp.bfloat16)


def join_exact(parts, count):
    parts = parts.astype(jnp.float32)
    return (parts[:, :count] + parts[:, count : 2 * count]) + parts[:, 2 * count : 3 * count]


def body(
    residual, attn_out, out_weight, post_gain, gate_up, down, route_ids, route_weight, final_gain
):
    row_count, model_width = residual.shape
    ep_size = lax.axis_size("ep")
    me = lax.axis_index("ep")
    local_experts = gate_up.shape[0]
    slice_width = out_weight.shape[0]
    half = row_count // 2
    ring = ring_order(ep_size)
    ring_index = jnp.array(ring, dtype=jnp.int32)
    pos = jnp.array([ring.index(p) for p in range(ep_size)], dtype=jnp.int32)[me]

    with jax.named_scope("route_weights"):
        expert_ids = jnp.arange(local_experts * ep_size, dtype=jnp.int32)
        dense_weight = jnp.sum(
            jnp.where(route_ids[:, :, None] == expert_ids, route_weight[:, :, None], 0.0), axis=1
        )
        dense_weight = dense_weight.reshape(row_count, ep_size, local_experts)
        own_weight = lax.dynamic_index_in_dim(dense_weight, me, 1, keepdims=False)

    with jax.named_scope("column_exchange"):
        columns = attn_out.reshape(row_count, ep_size, slice_width)
        pad = (-3 * local_experts) % 128
        by_shift = {}
        shifts = []
        for k in range(1, ep_size):
            for shift in (k, ep_size - k):
                if shift not in shifts:
                    shifts.append(shift)
        for shift in shifts:
            target = ring_index[(pos + shift) % ep_size]
            payload = jnp.concatenate(
                [
                    lax.dynamic_index_in_dim(columns, target, 1, keepdims=False),
                    split_exact(lax.dynamic_index_in_dim(dense_weight, target, 1, keepdims=False)),
                    jnp.zeros((row_count, pad), jnp.bfloat16),
                ],
                axis=1,
            )
            pairs = [(ring[q], ring[(q + shift) % ep_size]) for q in range(ep_size)]
            by_shift[shift] = lax.ppermute(payload, "ep", pairs)

    def shift_rows(shift, rows):
        got = by_shift[shift][rows]
        return got[:, :slice_width], join_exact(got[:, slice_width:], local_experts)

    with jax.named_scope("out_projection"):
        pieces = []
        step_weights = []
        for step in range(ep_size - 1):
            cols_fwd, w_fwd = shift_rows(step + 1, slice(0, half))
            cols_bwd, w_bwd = shift_rows(ep_size - 1 - step, slice(half, row_count))
            part = jnp.dot(
                jnp.concatenate([cols_fwd, cols_bwd], axis=0),
                out_weight,
                preferred_element_type=jnp.float32,
            )
            pieces.append((part[:half], part[half:]))
            step_weights.append((w_fwd, w_bwd))
        own_columns = lax.dynamic_index_in_dim(columns, me, 1, keepdims=False)
        own_part = jnp.dot(own_columns, out_weight, preferred_element_type=jnp.float32)
        projected = ring_reduce_scatter_steps(pieces, own_part, ring)
        middle = (residual.astype(jnp.float32) + projected).astype(jnp.bfloat16)

    normed = rms_scale(middle.astype(jnp.float32), post_gain).astype(jnp.bfloat16)
    with jax.named_scope("dispatch_gather"):
        arrived = ring_all_gather(normed, ring, pos)

    with jax.named_scope("local_experts"):
        first = ep_size // 2
        chunks = [list(range(first)), list(range(first, ep_size - 1))]
        pieces = [None] * (ep_size - 1)
        own_mix = None
        for c, steps in enumerate(chunks):
            rows_in = []
            weights_in = []
            for step in steps:
                rows_in += list(arrived[step])
                weights_in += list(step_weights[step])
            if c == len(chunks) - 1:
                rows_in.append(normed)
                weights_in.append(own_weight)
            mixed = expert_mix(
                jnp.concatenate(rows_in, axis=0), jnp.concatenate(weights_in, axis=0), gate_up, down
            )
            for i, step in enumerate(steps):
                pieces[step] = (mixed[(2 * i) * half : (2 * i + 1) * half],
                                mixed[(2 * i + 1) * half : (2 * i + 2) * half])
            if c == len(chunks) - 1:
                own_mix = mixed[2 * len(steps) * half :]

    with jax.named_scope("combine_return"):
        combined = ring_reduce_scatter_steps(pieces, own_mix, ring)
    updated = middle.astype(jnp.float32) + combined
    return (updated.astype(jnp.bfloat16), rms_scale(updated, final_gain).astype(jnp.bfloat16))


def solution(mesh):
    in_specs = (
        P(("rep", "ep"), None),
        P(("rep", "ep"), None),
        P("ep", None),
        P(),
        P("ep", None, None),
        P("ep", None, None),
        P(("rep", "ep"), None),
        P(("rep", "ep"), None),
        P(),
    )
    out_specs = (P(("rep", "ep"), None), P(("rep", "ep"), None))
    return jax.shard_map(body, mesh=mesh, in_specs=in_specs, out_specs=out_specs, check_vma=False)
```

```python
import jax
import jax.numpy as jnp
from jax import lax
from jax.sharding import PartitionSpec as P


def rms_scale(values, scale_gain):
    mean_square = jnp.mean(values * values, axis=-1, keepdims=True)
    return values * lax.rsqrt(mean_square + 1e-06) * scale_gain


def ring_order(n):
    if n % 2:
        return list(range(n))
    return list(range(0, n, 2)) + list(range(n - 1, 0, -2))


def ring_all_gather(block, ring, pos):
    n = len(ring)
    half = block.shape[0] // 2
    forward = [(ring[q], ring[(q + 1) % n]) for q in range(n)]
    backward = [(ring[q], ring[(q - 1) % n]) for q in range(n)]
    got_fwd, got_bwd = block[:half], block[half:]
    arrived = []
    for step in range(n - 1):
        got_fwd, got_bwd = lax.optimization_barrier(
            (lax.ppermute(got_fwd, "ep", forward), lax.ppermute(got_bwd, "ep", backward))
        )
        arrived.append((got_fwd, got_bwd))
    return arrived


def ring_reduce_scatter_steps(pieces, own, ring):
    n = len(ring)
    forward = [(ring[q], ring[(q + 1) % n]) for q in range(n)]
    backward = [(ring[q], ring[(q - 1) % n]) for q in range(n)]
    got_fwd = got_bwd = None
    for step in range(n - 1):
        send_fwd, send_bwd = pieces[step]
        if step:
            send_fwd = send_fwd + got_fwd
            send_bwd = send_bwd + got_bwd
        send_fwd, send_bwd = lax.optimization_barrier(
            (send_fwd.astype(jnp.bfloat16), send_bwd.astype(jnp.bfloat16))
        )
        got_fwd, got_bwd = lax.optimization_barrier(
            (lax.ppermute(send_fwd, "ep", forward), lax.ppermute(send_bwd, "ep", backward))
        )
        got_fwd = got_fwd.astype(jnp.float32)
        got_bwd = got_bwd.astype(jnp.float32)
    half = own.shape[0] // 2
    return jnp.concatenate([own[:half] + got_fwd, own[half:] + got_bwd], axis=0)


def expert_mix(rows, weights, gate_up, down):
    hidden_width = down.shape[1]
    total = None
    for e in range(gate_up.shape[0]):
        projected_up = jnp.dot(rows, gate_up[e], preferred_element_type=jnp.float32)
        activated = (
            jax.nn.silu(projected_up[:, :hidden_width]) * projected_up[:, hidden_width:]
        ).astype(jnp.bfloat16)
        expert_out = jnp.dot(activated, down[e], preferred_element_type=jnp.float32).astype(
            jnp.bfloat16
        )
        term = weights[:, e : e + 1] * expert_out.astype(jnp.float32)
        total = term if total is None else total + term
    return total


def split_exact(values):
    first = lax.reduce_precision(values, exponent_bits=8, mantissa_bits=7)
    rest = values - first
    second = lax.reduce_precision(rest, exponent_bits=8, mantissa_bits=7)
    third = rest - second
    return jnp.concatenate([first, second, third], axis=-1).astype(jnp.bfloat16)


def join_exact(parts, count):
    parts = parts.astype(jnp.float32)
    return (parts[:, :count] + parts[:, count : 2 * count]) + parts[:, 2 * count : 3 * count]


def body(
    residual, attn_out, out_weight, post_gain, gate_up, down, route_ids, route_weight, final_gain
):
    row_count, model_width = residual.shape
    ep_size = lax.axis_size("ep")
    me = lax.axis_index("ep")
    local_experts = gate_up.shape[0]
    slice_width = out_weight.shape[0]
    half = row_count // 2
    ring = ring_order(ep_size)
    ring_index = jnp.array(ring, dtype=jnp.int32)
    pos = jnp.array([ring.index(p) for p in range(ep_size)], dtype=jnp.int32)[me]

    with jax.named_scope("route_weights"):
        expert_ids = jnp.arange(local_experts * ep_size, dtype=jnp.int32)
        dense_weight = jnp.sum(
            jnp.where(route_ids[:, :, None] == expert_ids, route_weight[:, :, None], 0.0), axis=1
        )
        dense_weight = dense_weight.reshape(row_count, ep_size, local_experts)
        own_weight = lax.dynamic_index_in_dim(dense_weight, me, 1, keepdims=False)

    with jax.named_scope("column_exchange"):
        columns = attn_out.reshape(row_count, ep_size, slice_width)
        pad = (-3 * local_experts) % 128
        payloads = jnp.concatenate(
            [
                columns.transpose(1, 0, 2),
                split_exact(dense_weight).transpose(1, 0, 2),
                jnp.zeros((ep_size, row_count, pad), jnp.bfloat16),
            ],
            axis=2,
        )
        by_shift = {}
        shifts = []
        for k in range(1, ep_size):
            for shift in (k, ep_size - k):
                if shift not in shifts:
                    shifts.append(shift)
        for shift in shifts:
            target = ring_index[(pos + shift) % ep_size]
            payload = lax.dynamic_index_in_dim(payloads, target, 0, keepdims=False)
            pairs = [(ring[q], ring[(q + shift) % ep_size]) for q in range(ep_size)]
            by_shift[shift] = lax.ppermute(payload, "ep", pairs)

    def shift_rows(shift, rows):
        got = by_shift[shift][rows]
        return got[:, :slice_width], join_exact(got[:, slice_width:], local_experts)

    with jax.named_scope("out_projection"):
        pieces = []
        step_weights = []
        for step in range(ep_size - 1):
            cols_fwd, w_fwd = shift_rows(step + 1, slice(0, half))
            cols_bwd, w_bwd = shift_rows(ep_size - 1 - step, slice(half, row_count))
            part = jnp.dot(
                jnp.concatenate([cols_fwd, cols_bwd], axis=0),
                out_weight,
                preferred_element_type=jnp.float32,
            )
            pieces.append((part[:half], part[half:]))
            step_weights.append((w_fwd, w_bwd))
        own_columns = lax.dynamic_index_in_dim(columns, me, 1, keepdims=False)
        own_part = jnp.dot(own_columns, out_weight, preferred_element_type=jnp.float32)
        projected = ring_reduce_scatter_steps(pieces, own_part, ring)
        middle = (residual.astype(jnp.float32) + projected).astype(jnp.bfloat16)

    normed = rms_scale(middle.astype(jnp.float32), post_gain).astype(jnp.bfloat16)
    with jax.named_scope("dispatch_gather"):
        arrived = ring_all_gather(normed, ring, pos)

    with jax.named_scope("local_experts"):
        first = ep_size // 2
        chunks = [list(range(first)), list(range(first, ep_size - 1))]
        pieces = [None] * (ep_size - 1)
        own_mix = None
        for c, steps in enumerate(chunks):
            rows_in = []
            weights_in = []
            for step in steps:
                rows_in += list(arrived[step])
                weights_in += list(step_weights[step])
            if c == len(chunks) - 1:
                rows_in.append(normed)
                weights_in.append(own_weight)
            mixed = expert_mix(
                jnp.concatenate(rows_in, axis=0), jnp.concatenate(weights_in, axis=0), gate_up, down
            )
            for i, step in enumerate(steps):
                pieces[step] = (mixed[(2 * i) * half : (2 * i + 1) * half],
                                mixed[(2 * i + 1) * half : (2 * i + 2) * half])
            if c == len(chunks) - 1:
                own_mix = mixed[2 * len(steps) * half :]

    with jax.named_scope("combine_return"):
        combined = ring_reduce_scatter_steps(pieces, own_mix, ring)
    updated = middle.astype(jnp.float32) + combined
    return (updated.astype(jnp.bfloat16), rms_scale(updated, final_gain).astype(jnp.bfloat16))


def solution(mesh):
    in_specs = (
        P(("rep", "ep"), None),
        P(("rep", "ep"), None),
        P("ep", None),
        P(),
        P("ep", None, None),
        P("ep", None, None),
        P(("rep", "ep"), None),
        P(("rep", "ep"), None),
        P(),
    )
    out_specs = (P(("rep", "ep"), None), P(("rep", "ep"), None))
    return jax.shard_map(body, mesh=mesh, in_specs=in_specs, out_specs=out_specs, check_vma=False)
```

```python
import jax
import jax.numpy as jnp
from jax import lax
from jax.sharding import PartitionSpec as P


def rms_scale(values, scale_gain):
    mean_square = jnp.mean(values * values, axis=-1, keepdims=True)
    return values * lax.rsqrt(mean_square + 1e-06) * scale_gain


def ring_order(n):
    if n % 2:
        return list(range(n))
    return list(range(0, n, 2)) + list(range(n - 1, 0, -2))


def ring_reduce_scatter(blocks, ring, pos):
    n, rows, _ = blocks.shape
    half = rows // 2
    ring_index = jnp.array(ring, dtype=jnp.int32)
    forward = [(ring[q], ring[(q + 1) % n]) for q in range(n)]
    backward = [(ring[q], ring[(q - 1) % n]) for q in range(n)]
    got_fwd = got_bwd = None
    for step in range(n - 1):
        owner_fwd = ring_index[(pos - 1 - step) % n]
        owner_bwd = ring_index[(pos + 1 + step) % n]
        send_fwd = lax.dynamic_index_in_dim(blocks, owner_fwd, 0, keepdims=False)[:half]
        send_bwd = lax.dynamic_index_in_dim(blocks, owner_bwd, 0, keepdims=False)[half:]
        if step:
            send_fwd = send_fwd + got_fwd
            send_bwd = send_bwd + got_bwd
        send_fwd, send_bwd = lax.optimization_barrier(
            (send_fwd.astype(jnp.bfloat16), send_bwd.astype(jnp.bfloat16))
        )
        got_fwd, got_bwd = lax.optimization_barrier(
            (lax.ppermute(send_fwd, "ep", forward), lax.ppermute(send_bwd, "ep", backward))
        )
        got_fwd = got_fwd.astype(jnp.float32)
        got_bwd = got_bwd.astype(jnp.float32)
    me = ring_index[pos]
    own = lax.dynamic_index_in_dim(blocks, me, 0, keepdims=False)
    return jnp.concatenate([own[:half] + got_fwd, own[half:] + got_bwd], axis=0)


def ring_all_gather(block, ring, pos):
    n = len(ring)
    half = block.shape[0] // 2
    forward = [(ring[q], ring[(q + 1) % n]) for q in range(n)]
    backward = [(ring[q], ring[(q - 1) % n]) for q in range(n)]
    got_fwd, got_bwd = block[:half], block[half:]
    arrived = []
    for step in range(n - 1):
        got_fwd, got_bwd = lax.optimization_barrier(
            (lax.ppermute(got_fwd, "ep", forward), lax.ppermute(got_bwd, "ep", backward))
        )
        arrived.append((got_fwd, got_bwd))
    return arrived


def ring_reduce_scatter_steps(pieces, own, ring):
    n = len(ring)
    forward = [(ring[q], ring[(q + 1) % n]) for q in range(n)]
    backward = [(ring[q], ring[(q - 1) % n]) for q in range(n)]
    got_fwd = got_bwd = None
    for step in range(n - 1):
        send_fwd, send_bwd = pieces[step]
        if step:
            send_fwd = send_fwd + got_fwd
            send_bwd = send_bwd + got_bwd
        send_fwd, send_bwd = lax.optimization_barrier(
            (send_fwd.astype(jnp.bfloat16), send_bwd.astype(jnp.bfloat16))
        )
        got_fwd, got_bwd = lax.optimization_barrier(
            (lax.ppermute(send_fwd, "ep", forward), lax.ppermute(send_bwd, "ep", backward))
        )
        got_fwd = got_fwd.astype(jnp.float32)
        got_bwd = got_bwd.astype(jnp.float32)
    half = own.shape[0] // 2
    return jnp.concatenate([own[:half] + got_fwd, own[half:] + got_bwd], axis=0)


def expert_mix(rows, weights, gate_up, down):
    hidden_width = down.shape[1]
    total = None
    for e in range(gate_up.shape[0]):
        projected_up = jnp.dot(rows, gate_up[e], preferred_element_type=jnp.float32)
        activated = (
            jax.nn.silu(projected_up[:, :hidden_width]) * projected_up[:, hidden_width:]
        ).astype(jnp.bfloat16)
        expert_out = jnp.dot(activated, down[e], preferred_element_type=jnp.float32).astype(
            jnp.bfloat16
        )
        term = weights[:, e : e + 1] * expert_out.astype(jnp.float32)
        total = term if total is None else total + term
    return total


def split_exact(values):
    first = lax.reduce_precision(values, exponent_bits=8, mantissa_bits=7)
    rest = values - first
    second = lax.reduce_precision(rest, exponent_bits=8, mantissa_bits=7)
    third = rest - second
    return jnp.concatenate([first, second, third], axis=-1).astype(jnp.bfloat16)


def join_exact(parts, count):
    parts = parts.astype(jnp.float32)
    return (parts[..., :count] + parts[..., count : 2 * count]) + parts[..., 2 * count : 3 * count]


def body(
    residual, attn_out, out_weight, post_gain, gate_up, down, route_ids, route_weight, final_gain
):
    row_count, model_width = residual.shape
    ep_size = lax.axis_size("ep")
    me = lax.axis_index("ep")
    local_experts = gate_up.shape[0]
    hidden_width = down.shape[1]
    slice_width = out_weight.shape[0]
    group_rows = row_count * ep_size
    ring = ring_order(ep_size)
    pos = jnp.array([ring.index(p) for p in range(ep_size)], dtype=jnp.int32)[me]

    with jax.named_scope("route_weights"):
        expert_ids = jnp.arange(local_experts * ep_size, dtype=jnp.int32)
        dense_weight = jnp.sum(
            jnp.where(route_ids[:, :, None] == expert_ids, route_weight[:, :, None], 0.0), axis=1
        )
        dense_weight = dense_weight.reshape(row_count, ep_size, local_experts)

    with jax.named_scope("out_projection"):
        pad = (-3 * local_experts) % 128
        payloads = jnp.concatenate(
            [
                attn_out.reshape(row_count, ep_size, slice_width).transpose(1, 0, 2),
                split_exact(dense_weight).transpose(1, 0, 2),
                jnp.zeros((ep_size, row_count, pad), jnp.bfloat16),
            ],
            axis=2,
        )
        payloads = lax.all_to_all(payloads, "ep", split_axis=0, concat_axis=0, tiled=True)
        columns = payloads[:, :, :slice_width]
        row_weights = join_exact(payloads[:, :, slice_width : slice_width + 3 * local_experts],
                                 local_experts).reshape(group_rows, local_experts)
        partial = jnp.dot(
            columns.reshape(group_rows, slice_width), out_weight, preferred_element_type=jnp.float32
        )
        projected = ring_reduce_scatter(partial.reshape(ep_size, row_count, model_width), ring, pos)
        middle = (residual.astype(jnp.float32) + projected).astype(jnp.bfloat16)

    normed = rms_scale(middle.astype(jnp.float32), post_gain).astype(jnp.bfloat16)
    with jax.named_scope("dispatch_gather"):
        arrived = ring_all_gather(normed, ring, pos)

    ring_index = jnp.array(ring, dtype=jnp.int32)
    weight_blocks = row_weights.reshape(ep_size, row_count, local_experts)
    half = row_count // 2

    def step_weights(step):
        owner_fwd = ring_index[(pos - 1 - step) % ep_size]
        owner_bwd = ring_index[(pos + 1 + step) % ep_size]
        w_fwd = lax.dynamic_index_in_dim(weight_blocks, owner_fwd, 0, keepdims=False)[:half]
        w_bwd = lax.dynamic_index_in_dim(weight_blocks, owner_bwd, 0, keepdims=False)[half:]
        return w_fwd, w_bwd

    with jax.named_scope("local_experts"):
        first = (ep_size - 1 + 1) // 2
        chunks = [list(range(first)), list(range(first, ep_size - 1))]
        pieces = [None] * (ep_size - 1)
        own_part = None
        for c, steps in enumerate(chunks):
            rows_in = []
            weights_in = []
            for step in steps:
                rows_in += list(arrived[step])
                weights_in += list(step_weights(step))
            if c == len(chunks) - 1:
                rows_in.append(normed)
                weights_in.append(lax.dynamic_index_in_dim(weight_blocks, me, 0, keepdims=False))
            mixed = expert_mix(
                jnp.concatenate(rows_in, axis=0), jnp.concatenate(weights_in, axis=0), gate_up, down
            )
            for i, step in enumerate(steps):
                pieces[step] = (mixed[(2 * i) * half : (2 * i + 1) * half],
                                mixed[(2 * i + 1) * half : (2 * i + 2) * half])
            if c == len(chunks) - 1:
                own_part = mixed[2 * len(steps) * half :]

    with jax.named_scope("combine_return"):
        combined = ring_reduce_scatter_steps(pieces, own_part, ring)
    updated = middle.astype(jnp.float32) + combined
    return (updated.astype(jnp.bfloat16), rms_scale(updated, final_gain).astype(jnp.bfloat16))


def solution(mesh):
    in_specs = (
        P(("rep", "ep"), None),
        P(("rep", "ep"), None),
        P("ep", None),
        P(),
        P("ep", None, None),
        P("ep", None, None),
        P(("rep", "ep"), None),
        P(("rep", "ep"), None),
        P(),
    )
    out_specs = (P(("rep", "ep"), None), P(("rep", "ep"), None))
    return jax.shard_map(body, mesh=mesh, in_specs=in_specs, out_specs=out_specs, check_vma=False)
```

```python
import jax
import jax.numpy as jnp
from jax import lax
from jax.sharding import PartitionSpec as P


def rms_scale(values, scale_gain):
    mean_square = jnp.mean(values * values, axis=-1, keepdims=True)
    return values * lax.rsqrt(mean_square + 1e-06) * scale_gain


def ring_order(n):
    if n % 2:
        return list(range(n))
    return list(range(0, n, 2)) + list(range(n - 1, 0, -2))


def ring_reduce_scatter(blocks, ring, pos):
    n, rows, _ = blocks.shape
    half = rows // 2
    ring_index = jnp.array(ring, dtype=jnp.int32)
    forward = [(ring[q], ring[(q + 1) % n]) for q in range(n)]
    backward = [(ring[q], ring[(q - 1) % n]) for q in range(n)]
    got_fwd = got_bwd = None
    for step in range(n - 1):
        owner_fwd = ring_index[(pos - 1 - step) % n]
        owner_bwd = ring_index[(pos + 1 + step) % n]
        send_fwd = lax.dynamic_index_in_dim(blocks, owner_fwd, 0, keepdims=False)[:half]
        send_bwd = lax.dynamic_index_in_dim(blocks, owner_bwd, 0, keepdims=False)[half:]
        if step:
            send_fwd = send_fwd + got_fwd
            send_bwd = send_bwd + got_bwd
        send_fwd, send_bwd = lax.optimization_barrier(
            (send_fwd.astype(jnp.bfloat16), send_bwd.astype(jnp.bfloat16))
        )
        got_fwd, got_bwd = lax.optimization_barrier(
            (lax.ppermute(send_fwd, "ep", forward), lax.ppermute(send_bwd, "ep", backward))
        )
        got_fwd = got_fwd.astype(jnp.float32)
        got_bwd = got_bwd.astype(jnp.float32)
    me = ring_index[pos]
    own = lax.dynamic_index_in_dim(blocks, me, 0, keepdims=False)
    return jnp.concatenate([own[:half] + got_fwd, own[half:] + got_bwd], axis=0)


def ring_all_gather(block, ring, pos):
    n = len(ring)
    half = block.shape[0] // 2
    forward = [(ring[q], ring[(q + 1) % n]) for q in range(n)]
    backward = [(ring[q], ring[(q - 1) % n]) for q in range(n)]
    got_fwd, got_bwd = block[:half], block[half:]
    arrived = []
    for step in range(n - 1):
        got_fwd, got_bwd = lax.optimization_barrier(
            (lax.ppermute(got_fwd, "ep", forward), lax.ppermute(got_bwd, "ep", backward))
        )
        arrived.append((got_fwd, got_bwd))
    return arrived


def ring_reduce_scatter_steps(pieces, own, ring):
    n = len(ring)
    forward = [(ring[q], ring[(q + 1) % n]) for q in range(n)]
    backward = [(ring[q], ring[(q - 1) % n]) for q in range(n)]
    got_fwd = got_bwd = None
    for step in range(n - 1):
        send_fwd, send_bwd = pieces[step]
        if step:
            send_fwd = send_fwd + got_fwd
            send_bwd = send_bwd + got_bwd
        send_fwd, send_bwd = lax.optimization_barrier(
            (send_fwd.astype(jnp.bfloat16), send_bwd.astype(jnp.bfloat16))
        )
        got_fwd, got_bwd = lax.optimization_barrier(
            (lax.ppermute(send_fwd, "ep", forward), lax.ppermute(send_bwd, "ep", backward))
        )
        got_fwd = got_fwd.astype(jnp.float32)
        got_bwd = got_bwd.astype(jnp.float32)
    half = own.shape[0] // 2
    return jnp.concatenate([own[:half] + got_fwd, own[half:] + got_bwd], axis=0)


def expert_mix(rows, weights, gate_up, down):
    hidden_width = down.shape[1]
    total = None
    for e in range(gate_up.shape[0]):
        projected_up = jnp.dot(rows, gate_up[e], preferred_element_type=jnp.float32)
        activated = (
            jax.nn.silu(projected_up[:, :hidden_width]) * projected_up[:, hidden_width:]
        ).astype(jnp.bfloat16)
        expert_out = jnp.dot(activated, down[e], preferred_element_type=jnp.float32).astype(
            jnp.bfloat16
        )
        term = weights[:, e : e + 1] * expert_out.astype(jnp.float32)
        total = term if total is None else total + term
    return total


def body(
    residual, attn_out, out_weight, post_gain, gate_up, down, route_ids, route_weight, final_gain
):
    row_count, model_width = residual.shape
    ep_size = lax.axis_size("ep")
    me = lax.axis_index("ep")
    local_experts = gate_up.shape[0]
    hidden_width = down.shape[1]
    slice_width = out_weight.shape[0]
    group_rows = row_count * ep_size
    ring = ring_order(ep_size)
    pos = jnp.array([ring.index(p) for p in range(ep_size)], dtype=jnp.int32)[me]

    with jax.named_scope("route_weights"):
        expert_ids = jnp.arange(local_experts * ep_size, dtype=jnp.int32)
        dense_weight = jnp.sum(
            jnp.where(route_ids[:, :, None] == expert_ids, route_weight[:, :, None], 0.0), axis=1
        )
        dense_weight = dense_weight.reshape(row_count, ep_size, local_experts).transpose(1, 0, 2)
        row_weights = lax.all_to_all(dense_weight, "ep", split_axis=0, concat_axis=0, tiled=True)
        row_weights = row_weights.reshape(group_rows, local_experts)

    with jax.named_scope("out_projection"):
        columns = attn_out.reshape(row_count, ep_size, slice_width).transpose(1, 0, 2)
        columns = lax.all_to_all(columns, "ep", split_axis=0, concat_axis=0, tiled=True)
        columns, row_weights = lax.optimization_barrier((columns, row_weights))
        partial = jnp.dot(
            columns.reshape(group_rows, slice_width), out_weight, preferred_element_type=jnp.float32
        )
        projected = ring_reduce_scatter(partial.reshape(ep_size, row_count, model_width), ring, pos)
        middle = (residual.astype(jnp.float32) + projected).astype(jnp.bfloat16)

    normed = rms_scale(middle.astype(jnp.float32), post_gain).astype(jnp.bfloat16)
    with jax.named_scope("dispatch_gather"):
        arrived = ring_all_gather(normed, ring, pos)

    ring_index = jnp.array(ring, dtype=jnp.int32)
    weight_blocks = row_weights.reshape(ep_size, row_count, local_experts)
    half = row_count // 2

    def step_weights(step):
        owner_fwd = ring_index[(pos - 1 - step) % ep_size]
        owner_bwd = ring_index[(pos + 1 + step) % ep_size]
        w_fwd = lax.dynamic_index_in_dim(weight_blocks, owner_fwd, 0, keepdims=False)[:half]
        w_bwd = lax.dynamic_index_in_dim(weight_blocks, owner_bwd, 0, keepdims=False)[half:]
        return w_fwd, w_bwd

    with jax.named_scope("local_experts"):
        steps_all = list(range(ep_size - 1))
        chunks = [steps_all[i : i + 2] for i in range(0, ep_size - 1, 2)]
        pieces = [None] * (ep_size - 1)
        own_part = None
        for c, steps in enumerate(chunks):
            rows_in = []
            weights_in = []
            for step in steps:
                rows_in += list(arrived[step])
                weights_in += list(step_weights(step))
            if c == len(chunks) - 1:
                rows_in.append(normed)
                weights_in.append(lax.dynamic_index_in_dim(weight_blocks, me, 0, keepdims=False))
            mixed = expert_mix(
                jnp.concatenate(rows_in, axis=0), jnp.concatenate(weights_in, axis=0), gate_up, down
            )
            for i, step in enumerate(steps):
                pieces[step] = (mixed[(2 * i) * half : (2 * i + 1) * half],
                                mixed[(2 * i + 1) * half : (2 * i + 2) * half])
            if c == len(chunks) - 1:
                own_part = mixed[2 * len(steps) * half :]

    with jax.named_scope("combine_return"):
        combined = ring_reduce_scatter_steps(pieces, own_part, ring)
    updated = middle.astype(jnp.float32) + combined
    return (updated.astype(jnp.bfloat16), rms_scale(updated, final_gain).astype(jnp.bfloat16))


def solution(mesh):
    in_specs = (
        P(("rep", "ep"), None),
        P(("rep", "ep"), None),
        P("ep", None),
        P(),
        P("ep", None, None),
        P("ep", None, None),
        P(("rep", "ep"), None),
        P(("rep", "ep"), None),
        P(),
    )
    out_specs = (P(("rep", "ep"), None), P(("rep", "ep"), None))
    return jax.shard_map(body, mesh=mesh, in_specs=in_specs, out_specs=out_specs, check_vma=False)
```

```python
import jax
import jax.numpy as jnp
from jax import lax
from jax.sharding import PartitionSpec as P


def rms_scale(values, scale_gain):
    mean_square = jnp.mean(values * values, axis=-1, keepdims=True)
    return values * lax.rsqrt(mean_square + 1e-06) * scale_gain


def ring_order(n):
    if n % 2:
        return list(range(n))
    return list(range(0, n, 2)) + list(range(n - 1, 0, -2))


def ring_reduce_scatter(blocks, ring, pos):
    n, rows, _ = blocks.shape
    half = rows // 2
    ring_index = jnp.array(ring, dtype=jnp.int32)
    forward = [(ring[q], ring[(q + 1) % n]) for q in range(n)]
    backward = [(ring[q], ring[(q - 1) % n]) for q in range(n)]
    got_fwd = got_bwd = None
    for step in range(n - 1):
        owner_fwd = ring_index[(pos - 1 - step) % n]
        owner_bwd = ring_index[(pos + 1 + step) % n]
        send_fwd = lax.dynamic_index_in_dim(blocks, owner_fwd, 0, keepdims=False)[:half]
        send_bwd = lax.dynamic_index_in_dim(blocks, owner_bwd, 0, keepdims=False)[half:]
        if step:
            send_fwd = send_fwd + got_fwd
            send_bwd = send_bwd + got_bwd
        send_fwd, send_bwd = lax.optimization_barrier(
            (send_fwd.astype(jnp.bfloat16), send_bwd.astype(jnp.bfloat16))
        )
        got_fwd, got_bwd = lax.optimization_barrier(
            (lax.ppermute(send_fwd, "ep", forward), lax.ppermute(send_bwd, "ep", backward))
        )
        got_fwd = got_fwd.astype(jnp.float32)
        got_bwd = got_bwd.astype(jnp.float32)
    me = ring_index[pos]
    own = lax.dynamic_index_in_dim(blocks, me, 0, keepdims=False)
    return jnp.concatenate([own[:half] + got_fwd, own[half:] + got_bwd], axis=0)


def ring_all_gather(block, ring, pos):
    n = len(ring)
    half = block.shape[0] // 2
    forward = [(ring[q], ring[(q + 1) % n]) for q in range(n)]
    backward = [(ring[q], ring[(q - 1) % n]) for q in range(n)]
    got_fwd, got_bwd = block[:half], block[half:]
    arrived = []
    for step in range(n - 1):
        got_fwd, got_bwd = lax.optimization_barrier(
            (lax.ppermute(got_fwd, "ep", forward), lax.ppermute(got_bwd, "ep", backward))
        )
        arrived.append((got_fwd, got_bwd))
    return arrived


def ring_reduce_scatter_steps(pieces, own, ring):
    n = len(ring)
    forward = [(ring[q], ring[(q + 1) % n]) for q in range(n)]
    backward = [(ring[q], ring[(q - 1) % n]) for q in range(n)]
    got_fwd = got_bwd = None
    for step in range(n - 1):
        send_fwd, send_bwd = pieces[step]
        if step:
            send_fwd = send_fwd + got_fwd
            send_bwd = send_bwd + got_bwd
        send_fwd, send_bwd = lax.optimization_barrier(
            (send_fwd.astype(jnp.bfloat16), send_bwd.astype(jnp.bfloat16))
        )
        got_fwd, got_bwd = lax.optimization_barrier(
            (lax.ppermute(send_fwd, "ep", forward), lax.ppermute(send_bwd, "ep", backward))
        )
        got_fwd = got_fwd.astype(jnp.float32)
        got_bwd = got_bwd.astype(jnp.float32)
    half = own.shape[0] // 2
    return jnp.concatenate([own[:half] + got_fwd, own[half:] + got_bwd], axis=0)


def expert_mix(rows, weights, gate_up, down):
    hidden_width = down.shape[1]
    total = None
    for e in range(gate_up.shape[0]):
        projected_up = jnp.dot(rows, gate_up[e], preferred_element_type=jnp.float32)
        activated = (
            jax.nn.silu(projected_up[:, :hidden_width]) * projected_up[:, hidden_width:]
        ).astype(jnp.bfloat16)
        expert_out = jnp.dot(activated, down[e], preferred_element_type=jnp.float32).astype(
            jnp.bfloat16
        )
        term = weights[:, e : e + 1] * expert_out.astype(jnp.float32)
        total = term if total is None else total + term
    return total


def split_exact(values):
    first = lax.reduce_precision(values, exponent_bits=8, mantissa_bits=7)
    rest = values - first
    second = lax.reduce_precision(rest, exponent_bits=8, mantissa_bits=7)
    third = rest - second
    return jnp.concatenate([first, second, third], axis=-1).astype(jnp.bfloat16)


def join_exact(parts, count):
    parts = parts.astype(jnp.float32)
    return (parts[..., :count] + parts[..., count : 2 * count]) + parts[..., 2 * count : 3 * count]


def body(
    residual, attn_out, out_weight, post_gain, gate_up, down, route_ids, route_weight, final_gain
):
    row_count, model_width = residual.shape
    ep_size = lax.axis_size("ep")
    me = lax.axis_index("ep")
    local_experts = gate_up.shape[0]
    hidden_width = down.shape[1]
    slice_width = out_weight.shape[0]
    group_rows = row_count * ep_size
    ring = ring_order(ep_size)
    pos = jnp.array([ring.index(p) for p in range(ep_size)], dtype=jnp.int32)[me]

    with jax.named_scope("route_weights"):
        experts = local_experts * ep_size
        expert_ids = jnp.arange(experts, dtype=jnp.int32)
        dense_weight = jnp.sum(
            jnp.where(route_ids[:, :, None] == expert_ids, route_weight[:, :, None], 0.0), axis=1
        )
        own_weight = lax.dynamic_index_in_dim(
            dense_weight.reshape(row_count, ep_size, local_experts), me, 1, keepdims=False
        )

    with jax.named_scope("out_projection"):
        columns = attn_out.reshape(row_count, ep_size, slice_width).transpose(1, 0, 2)
        columns = lax.all_to_all(columns, "ep", split_axis=0, concat_axis=0, tiled=True)
        partial = jnp.dot(
            columns.reshape(group_rows, slice_width), out_weight, preferred_element_type=jnp.float32
        )
        projected = ring_reduce_scatter(partial.reshape(ep_size, row_count, model_width), ring, pos)
        middle = (residual.astype(jnp.float32) + projected).astype(jnp.bfloat16)

    normed = rms_scale(middle.astype(jnp.float32), post_gain).astype(jnp.bfloat16)
    with jax.named_scope("dispatch_gather"):
        pad = (-3 * experts) % 128
        payload = jnp.concatenate(
            [normed, split_exact(dense_weight), jnp.zeros((row_count, pad), jnp.bfloat16)], axis=1
        )
        arrived = ring_all_gather(payload, ring, pos)

    def unpack(piece):
        weights = join_exact(piece[:, model_width : model_width + 3 * experts], experts)
        weights = lax.dynamic_index_in_dim(
            weights.reshape(-1, ep_size, local_experts), me, 1, keepdims=False
        )
        return piece[:, :model_width], weights

    half = row_count // 2

    with jax.named_scope("local_experts"):
        steps_all = list(range(ep_size - 1))
        chunks = [steps_all[i : i + 2] for i in range(0, ep_size - 1, 2)]
        pieces = [None] * (ep_size - 1)
        own_part = None
        for c, steps in enumerate(chunks):
            rows_in = []
            weights_in = []
            for step in steps:
                for piece in arrived[step]:
                    piece_rows, piece_weights = unpack(piece)
                    rows_in.append(piece_rows)
                    weights_in.append(piece_weights)
            if c == len(chunks) - 1:
                rows_in.append(normed)
                weights_in.append(own_weight)
            mixed = expert_mix(
                jnp.concatenate(rows_in, axis=0), jnp.concatenate(weights_in, axis=0), gate_up, down
            )
            for i, step in enumerate(steps):
                pieces[step] = (mixed[(2 * i) * half : (2 * i + 1) * half],
                                mixed[(2 * i + 1) * half : (2 * i + 2) * half])
            if c == len(chunks) - 1:
                own_part = mixed[2 * len(steps) * half :]

    with jax.named_scope("combine_return"):
        combined = ring_reduce_scatter_steps(pieces, own_part, ring)
    updated = middle.astype(jnp.float32) + combined
    return (updated.astype(jnp.bfloat16), rms_scale(updated, final_gain).astype(jnp.bfloat16))


def solution(mesh):
    in_specs = (
        P(("rep", "ep"), None),
        P(("rep", "ep"), None),
        P("ep", None),
        P(),
        P("ep", None, None),
        P("ep", None, None),
        P(("rep", "ep"), None),
        P(("rep", "ep"), None),
        P(),
    )
    out_specs = (P(("rep", "ep"), None), P(("rep", "ep"), None))
    return jax.shard_map(body, mesh=mesh, in_specs=in_specs, out_specs=out_specs, check_vma=False)
```

```python
import jax
import jax.numpy as jnp
from jax import lax
from jax.sharding import PartitionSpec as P


def rms_scale(values, scale_gain):
    mean_square = jnp.mean(values * values, axis=-1, keepdims=True)
    return values * lax.rsqrt(mean_square + 1e-06) * scale_gain


def ring_order(n):
    if n % 2:
        return list(range(n))
    return list(range(0, n, 2)) + list(range(n - 1, 0, -2))


def ring_reduce_scatter(blocks, ring, pos):
    n, rows, _ = blocks.shape
    half = rows // 2
    ring_index = jnp.array(ring, dtype=jnp.int32)
    forward = [(ring[q], ring[(q + 1) % n]) for q in range(n)]
    backward = [(ring[q], ring[(q - 1) % n]) for q in range(n)]
    got_fwd = got_bwd = None
    for step in range(n - 1):
        owner_fwd = ring_index[(pos - 1 - step) % n]
        owner_bwd = ring_index[(pos + 1 + step) % n]
        send_fwd = lax.dynamic_index_in_dim(blocks, owner_fwd, 0, keepdims=False)[:half]
        send_bwd = lax.dynamic_index_in_dim(blocks, owner_bwd, 0, keepdims=False)[half:]
        if step:
            send_fwd = send_fwd + got_fwd
            send_bwd = send_bwd + got_bwd
        send_fwd, send_bwd = lax.optimization_barrier(
            (send_fwd.astype(jnp.bfloat16), send_bwd.astype(jnp.bfloat16))
        )
        got_fwd, got_bwd = lax.optimization_barrier(
            (lax.ppermute(send_fwd, "ep", forward), lax.ppermute(send_bwd, "ep", backward))
        )
        got_fwd = got_fwd.astype(jnp.float32)
        got_bwd = got_bwd.astype(jnp.float32)
    me = ring_index[pos]
    own = lax.dynamic_index_in_dim(blocks, me, 0, keepdims=False)
    return jnp.concatenate([own[:half] + got_fwd, own[half:] + got_bwd], axis=0)


def ring_all_gather(block, ring, pos):
    n = len(ring)
    half = block.shape[0] // 2
    forward = [(ring[q], ring[(q + 1) % n]) for q in range(n)]
    backward = [(ring[q], ring[(q - 1) % n]) for q in range(n)]
    got_fwd, got_bwd = block[:half], block[half:]
    arrived = []
    for step in range(n - 1):
        got_fwd, got_bwd = lax.optimization_barrier(
            (lax.ppermute(got_fwd, "ep", forward), lax.ppermute(got_bwd, "ep", backward))
        )
        arrived.append((got_fwd, got_bwd))
    return arrived


def ring_reduce_scatter_steps(pieces, own, ring):
    n = len(ring)
    forward = [(ring[q], ring[(q + 1) % n]) for q in range(n)]
    backward = [(ring[q], ring[(q - 1) % n]) for q in range(n)]
    got_fwd = got_bwd = None
    for step in range(n - 1):
        send_fwd, send_bwd = pieces[step]
        if step:
            send_fwd = send_fwd + got_fwd
            send_bwd = send_bwd + got_bwd
        send_fwd, send_bwd = lax.optimization_barrier(
            (send_fwd.astype(jnp.bfloat16), send_bwd.astype(jnp.bfloat16))
        )
        got_fwd, got_bwd = lax.optimization_barrier(
            (lax.ppermute(send_fwd, "ep", forward), lax.ppermute(send_bwd, "ep", backward))
        )
        got_fwd = got_fwd.astype(jnp.float32)
        got_bwd = got_bwd.astype(jnp.float32)
    half = own.shape[0] // 2
    return jnp.concatenate([own[:half] + got_fwd, own[half:] + got_bwd], axis=0)


def expert_mix(rows, weights, gate_up, down):
    hidden_width = down.shape[1]
    total = None
    for e in range(gate_up.shape[0]):
        projected_up = jnp.dot(rows, gate_up[e], preferred_element_type=jnp.float32)
        activated = (
            jax.nn.silu(projected_up[:, :hidden_width]) * projected_up[:, hidden_width:]
        ).astype(jnp.bfloat16)
        expert_out = jnp.dot(activated, down[e], preferred_element_type=jnp.float32).astype(
            jnp.bfloat16
        )
        term = weights[:, e : e + 1] * expert_out.astype(jnp.float32)
        total = term if total is None else total + term
    return total


def body(
    residual, attn_out, out_weight, post_gain, gate_up, down, route_ids, route_weight, final_gain
):
    row_count, model_width = residual.shape
    ep_size = lax.axis_size("ep")
    me = lax.axis_index("ep")
    local_experts = gate_up.shape[0]
    hidden_width = down.shape[1]
    slice_width = out_weight.shape[0]
    group_rows = row_count * ep_size
    ring = ring_order(ep_size)
    pos = jnp.array([ring.index(p) for p in range(ep_size)], dtype=jnp.int32)[me]

    with jax.named_scope("route_weights"):
        expert_ids = jnp.arange(local_experts * ep_size, dtype=jnp.int32)
        dense_weight = jnp.sum(
            jnp.where(route_ids[:, :, None] == expert_ids, route_weight[:, :, None], 0.0), axis=1
        )
        dense_weight = dense_weight.reshape(row_count, ep_size, local_experts).transpose(1, 0, 2)

    with jax.named_scope("out_projection"):
        columns = attn_out.reshape(row_count, ep_size, slice_width).transpose(1, 0, 2)
        columns = lax.all_to_all(columns, "ep", split_axis=0, concat_axis=0, tiled=True)
        columns, dense_weight = lax.optimization_barrier((columns, dense_weight))
        row_weights = lax.all_to_all(dense_weight, "ep", split_axis=0, concat_axis=0, tiled=True)
        row_weights = row_weights.reshape(group_rows, local_experts)
        partial = jnp.dot(
            columns.reshape(group_rows, slice_width), out_weight, preferred_element_type=jnp.float32
        )
        projected = ring_reduce_scatter(partial.reshape(ep_size, row_count, model_width), ring, pos)
        middle = (residual.astype(jnp.float32) + projected).astype(jnp.bfloat16)

    normed = rms_scale(middle.astype(jnp.float32), post_gain).astype(jnp.bfloat16)
    with jax.named_scope("dispatch_gather"):
        arrived = ring_all_gather(normed, ring, pos)

    ring_index = jnp.array(ring, dtype=jnp.int32)
    weight_blocks = row_weights.reshape(ep_size, row_count, local_experts)
    half = row_count // 2

    def step_weights(step):
        owner_fwd = ring_index[(pos - 1 - step) % ep_size]
        owner_bwd = ring_index[(pos + 1 + step) % ep_size]
        w_fwd = lax.dynamic_index_in_dim(weight_blocks, owner_fwd, 0, keepdims=False)[:half]
        w_bwd = lax.dynamic_index_in_dim(weight_blocks, owner_bwd, 0, keepdims=False)[half:]
        return w_fwd, w_bwd

    with jax.named_scope("local_experts"):
        steps_all = list(range(ep_size - 1))
        chunks = [steps_all[i : i + 2] for i in range(0, ep_size - 1, 2)]
        pieces = [None] * (ep_size - 1)
        own_part = None
        for c, steps in enumerate(chunks):
            rows_in = []
            weights_in = []
            for step in steps:
                rows_in += list(arrived[step])
                weights_in += list(step_weights(step))
            if c == len(chunks) - 1:
                rows_in.append(normed)
                weights_in.append(lax.dynamic_index_in_dim(weight_blocks, me, 0, keepdims=False))
            mixed = expert_mix(
                jnp.concatenate(rows_in, axis=0), jnp.concatenate(weights_in, axis=0), gate_up, down
            )
            for i, step in enumerate(steps):
                pieces[step] = (mixed[(2 * i) * half : (2 * i + 1) * half],
                                mixed[(2 * i + 1) * half : (2 * i + 2) * half])
            if c == len(chunks) - 1:
                own_part = mixed[2 * len(steps) * half :]

    with jax.named_scope("combine_return"):
        combined = ring_reduce_scatter_steps(pieces, own_part, ring)
    updated = middle.astype(jnp.float32) + combined
    return (updated.astype(jnp.bfloat16), rms_scale(updated, final_gain).astype(jnp.bfloat16))


def solution(mesh):
    in_specs = (
        P(("rep", "ep"), None),
        P(("rep", "ep"), None),
        P("ep", None),
        P(),
        P("ep", None, None),
        P("ep", None, None),
        P(("rep", "ep"), None),
        P(("rep", "ep"), None),
        P(),
    )
    out_specs = (P(("rep", "ep"), None), P(("rep", "ep"), None))
    return jax.shard_map(body, mesh=mesh, in_specs=in_specs, out_specs=out_specs, check_vma=False)
```

```python
import jax
import jax.numpy as jnp
from jax import lax
from jax.sharding import PartitionSpec as P


def rms_scale(values, scale_gain):
    mean_square = jnp.mean(values * values, axis=-1, keepdims=True)
    return values * lax.rsqrt(mean_square + 1e-06) * scale_gain


def ring_order(n):
    if n % 2:
        return list(range(n))
    return list(range(0, n, 2)) + list(range(n - 1, 0, -2))


def ring_reduce_scatter(blocks, ring, pos):
    n, rows, _ = blocks.shape
    half = rows // 2
    ring_index = jnp.array(ring, dtype=jnp.int32)
    forward = [(ring[q], ring[(q + 1) % n]) for q in range(n)]
    backward = [(ring[q], ring[(q - 1) % n]) for q in range(n)]
    got_fwd = got_bwd = None
    for step in range(n - 1):
        owner_fwd = ring_index[(pos - 1 - step) % n]
        owner_bwd = ring_index[(pos + 1 + step) % n]
        send_fwd = lax.dynamic_index_in_dim(blocks, owner_fwd, 0, keepdims=False)[:half]
        send_bwd = lax.dynamic_index_in_dim(blocks, owner_bwd, 0, keepdims=False)[half:]
        if step:
            send_fwd = send_fwd + got_fwd
            send_bwd = send_bwd + got_bwd
        send_fwd, send_bwd = lax.optimization_barrier(
            (send_fwd.astype(jnp.bfloat16), send_bwd.astype(jnp.bfloat16))
        )
        got_fwd, got_bwd = lax.optimization_barrier(
            (lax.ppermute(send_fwd, "ep", forward), lax.ppermute(send_bwd, "ep", backward))
        )
        got_fwd = got_fwd.astype(jnp.float32)
        got_bwd = got_bwd.astype(jnp.float32)
    me = ring_index[pos]
    own = lax.dynamic_index_in_dim(blocks, me, 0, keepdims=False)
    return jnp.concatenate([own[:half] + got_fwd, own[half:] + got_bwd], axis=0)


def ring_all_gather(block, ring, pos):
    n = len(ring)
    half = block.shape[0] // 2
    forward = [(ring[q], ring[(q + 1) % n]) for q in range(n)]
    backward = [(ring[q], ring[(q - 1) % n]) for q in range(n)]
    got_fwd, got_bwd = block[:half], block[half:]
    arrived = []
    for step in range(n - 1):
        got_fwd, got_bwd = lax.optimization_barrier(
            (lax.ppermute(got_fwd, "ep", forward), lax.ppermute(got_bwd, "ep", backward))
        )
        arrived.append((got_fwd, got_bwd))
    return arrived


def ring_reduce_scatter_steps(pieces, own, ring):
    n = len(ring)
    forward = [(ring[q], ring[(q + 1) % n]) for q in range(n)]
    backward = [(ring[q], ring[(q - 1) % n]) for q in range(n)]
    got_fwd = got_bwd = None
    for step in range(n - 1):
        send_fwd, send_bwd = pieces[step]
        if step:
            send_fwd = send_fwd + got_fwd
            send_bwd = send_bwd + got_bwd
        send_fwd, send_bwd = lax.optimization_barrier(
            (send_fwd.astype(jnp.bfloat16), send_bwd.astype(jnp.bfloat16))
        )
        got_fwd, got_bwd = lax.optimization_barrier(
            (lax.ppermute(send_fwd, "ep", forward), lax.ppermute(send_bwd, "ep", backward))
        )
        got_fwd = got_fwd.astype(jnp.float32)
        got_bwd = got_bwd.astype(jnp.float32)
    half = own.shape[0] // 2
    return jnp.concatenate([own[:half] + got_fwd, own[half:] + got_bwd], axis=0)


def expert_mix(rows, weights, gate_up, down):
    hidden_width = down.shape[1]
    total = None
    for e in range(gate_up.shape[0]):
        projected_up = jnp.dot(rows, gate_up[e], preferred_element_type=jnp.float32)
        activated = (
            jax.nn.silu(projected_up[:, :hidden_width]) * projected_up[:, hidden_width:]
        ).astype(jnp.bfloat16)
        expert_out = jnp.dot(activated, down[e], preferred_element_type=jnp.float32).astype(
            jnp.bfloat16
        )
        term = weights[:, e : e + 1] * expert_out.astype(jnp.float32)
        total = term if total is None else total + term
    return total


def body(
    residual, attn_out, out_weight, post_gain, gate_up, down, route_ids, route_weight, final_gain
):
    row_count, model_width = residual.shape
    ep_size = lax.axis_size("ep")
    me = lax.axis_index("ep")
    local_experts = gate_up.shape[0]
    hidden_width = down.shape[1]
    slice_width = out_weight.shape[0]
    group_rows = row_count * ep_size
    ring = ring_order(ep_size)
    pos = jnp.array([ring.index(p) for p in range(ep_size)], dtype=jnp.int32)[me]

    with jax.named_scope("route_weights"):
        expert_ids = jnp.arange(local_experts * ep_size, dtype=jnp.int32)
        dense_weight = jnp.sum(
            jnp.where(route_ids[:, :, None] == expert_ids, route_weight[:, :, None], 0.0), axis=1
        )
        dense_weight = dense_weight.reshape(row_count, ep_size, local_experts).transpose(1, 0, 2)

    with jax.named_scope("out_projection"):
        columns = attn_out.reshape(row_count, ep_size, slice_width).transpose(1, 0, 2)
        columns, dense_weight = lax.optimization_barrier((columns, dense_weight))
        columns, row_weights = lax.optimization_barrier(
            (
                lax.all_to_all(columns, "ep", split_axis=0, concat_axis=0, tiled=True),
                lax.all_to_all(dense_weight, "ep", split_axis=0, concat_axis=0, tiled=True),
            )
        )
        row_weights = row_weights.reshape(group_rows, local_experts)
        partial = jnp.dot(
            columns.reshape(group_rows, slice_width), out_weight, preferred_element_type=jnp.float32
        )
        projected = ring_reduce_scatter(partial.reshape(ep_size, row_count, model_width), ring, pos)
        middle = (residual.astype(jnp.float32) + projected).astype(jnp.bfloat16)

    normed = rms_scale(middle.astype(jnp.float32), post_gain).astype(jnp.bfloat16)
    with jax.named_scope("dispatch_gather"):
        arrived = ring_all_gather(normed, ring, pos)

    ring_index = jnp.array(ring, dtype=jnp.int32)
    weight_blocks = row_weights.reshape(ep_size, row_count, local_experts)
    half = row_count // 2

    def step_weights(step):
        owner_fwd = ring_index[(pos - 1 - step) % ep_size]
        owner_bwd = ring_index[(pos + 1 + step) % ep_size]
        w_fwd = lax.dynamic_index_in_dim(weight_blocks, owner_fwd, 0, keepdims=False)[:half]
        w_bwd = lax.dynamic_index_in_dim(weight_blocks, owner_bwd, 0, keepdims=False)[half:]
        return w_fwd, w_bwd

    with jax.named_scope("local_experts"):
        steps_all = list(range(ep_size - 1))
        chunks = [steps_all[i : i + 2] for i in range(0, ep_size - 1, 2)]
        pieces = [None] * (ep_size - 1)
        own_part = None
        for c, steps in enumerate(chunks):
            rows_in = []
            weights_in = []
            for step in steps:
                rows_in += list(arrived[step])
                weights_in += list(step_weights(step))
            if c == len(chunks) - 1:
                rows_in.append(normed)
                weights_in.append(lax.dynamic_index_in_dim(weight_blocks, me, 0, keepdims=False))
            mixed = expert_mix(
                jnp.concatenate(rows_in, axis=0), jnp.concatenate(weights_in, axis=0), gate_up, down
            )
            for i, step in enumerate(steps):
                pieces[step] = (mixed[(2 * i) * half : (2 * i + 1) * half],
                                mixed[(2 * i + 1) * half : (2 * i + 2) * half])
            if c == len(chunks) - 1:
                own_part = mixed[2 * len(steps) * half :]

    with jax.named_scope("combine_return"):
        combined = ring_reduce_scatter_steps(pieces, own_part, ring)
    updated = middle.astype(jnp.float32) + combined
    return (updated.astype(jnp.bfloat16), rms_scale(updated, final_gain).astype(jnp.bfloat16))


def solution(mesh):
    in_specs = (
        P(("rep", "ep"), None),
        P(("rep", "ep"), None),
        P("ep", None),
        P(),
        P("ep", None, None),
        P("ep", None, None),
        P(("rep", "ep"), None),
        P(("rep", "ep"), None),
        P(),
    )
    out_specs = (P(("rep", "ep"), None), P(("rep", "ep"), None))
    return jax.shard_map(body, mesh=mesh, in_specs=in_specs, out_specs=out_specs, check_vma=False)
```

```python
import jax
import jax.numpy as jnp
from jax import lax
from jax.sharding import PartitionSpec as P


def rms_scale(values, scale_gain):
    mean_square = jnp.mean(values * values, axis=-1, keepdims=True)
    return values * lax.rsqrt(mean_square + 1e-06) * scale_gain


def ring_order(n):
    if n % 2:
        return list(range(n))
    return list(range(0, n, 2)) + list(range(n - 1, 0, -2))


def ring_reduce_scatter(blocks, ring, pos):
    n, rows, _ = blocks.shape
    half = rows // 2
    ring_index = jnp.array(ring, dtype=jnp.int32)
    forward = [(ring[q], ring[(q + 1) % n]) for q in range(n)]
    backward = [(ring[q], ring[(q - 1) % n]) for q in range(n)]
    got_fwd = got_bwd = None
    for step in range(n - 1):
        owner_fwd = ring_index[(pos - 1 - step) % n]
        owner_bwd = ring_index[(pos + 1 + step) % n]
        send_fwd = lax.dynamic_index_in_dim(blocks, owner_fwd, 0, keepdims=False)[:half]
        send_bwd = lax.dynamic_index_in_dim(blocks, owner_bwd, 0, keepdims=False)[half:]
        if step:
            send_fwd = send_fwd + got_fwd
            send_bwd = send_bwd + got_bwd
        send_fwd, send_bwd = lax.optimization_barrier(
            (send_fwd.astype(jnp.bfloat16), send_bwd.astype(jnp.bfloat16))
        )
        got_fwd, got_bwd = lax.optimization_barrier(
            (lax.ppermute(send_fwd, "ep", forward), lax.ppermute(send_bwd, "ep", backward))
        )
        got_fwd = got_fwd.astype(jnp.float32)
        got_bwd = got_bwd.astype(jnp.float32)
    me = ring_index[pos]
    own = lax.dynamic_index_in_dim(blocks, me, 0, keepdims=False)
    return jnp.concatenate([own[:half] + got_fwd, own[half:] + got_bwd], axis=0)


def ring_all_gather(block, ring, pos):
    n = len(ring)
    half = block.shape[0] // 2
    forward = [(ring[q], ring[(q + 1) % n]) for q in range(n)]
    backward = [(ring[q], ring[(q - 1) % n]) for q in range(n)]
    got_fwd, got_bwd = block[:half], block[half:]
    arrived = []
    for step in range(n - 1):
        got_fwd, got_bwd = lax.optimization_barrier(
            (lax.ppermute(got_fwd, "ep", forward), lax.ppermute(got_bwd, "ep", backward))
        )
        arrived.append((got_fwd, got_bwd))
    return arrived


def ring_reduce_scatter_steps(pieces, own, ring):
    n = len(ring)
    forward = [(ring[q], ring[(q + 1) % n]) for q in range(n)]
    backward = [(ring[q], ring[(q - 1) % n]) for q in range(n)]
    got_fwd = got_bwd = None
    for step in range(n - 1):
        send_fwd, send_bwd = pieces[step]
        if step:
            send_fwd = send_fwd + got_fwd
            send_bwd = send_bwd + got_bwd
        send_fwd, send_bwd = lax.optimization_barrier(
            (send_fwd.astype(jnp.bfloat16), send_bwd.astype(jnp.bfloat16))
        )
        got_fwd, got_bwd = lax.optimization_barrier(
            (lax.ppermute(send_fwd, "ep", forward), lax.ppermute(send_bwd, "ep", backward))
        )
        got_fwd = got_fwd.astype(jnp.float32)
        got_bwd = got_bwd.astype(jnp.float32)
    half = own.shape[0] // 2
    return jnp.concatenate([own[:half] + got_fwd, own[half:] + got_bwd], axis=0)


def expert_mix(rows, weights, gate_up, down):
    hidden_width = down.shape[1]
    total = None
    for e in range(gate_up.shape[0]):
        projected_up = jnp.dot(rows, gate_up[e], preferred_element_type=jnp.float32)
        activated = (
            jax.nn.silu(projected_up[:, :hidden_width]) * projected_up[:, hidden_width:]
        ).astype(jnp.bfloat16)
        expert_out = jnp.dot(activated, down[e], preferred_element_type=jnp.float32).astype(
            jnp.bfloat16
        )
        term = weights[:, e : e + 1] * expert_out.astype(jnp.float32)
        total = term if total is None else total + term
    return total


def body(
    residual, attn_out, out_weight, post_gain, gate_up, down, route_ids, route_weight, final_gain
):
    row_count, model_width = residual.shape
    ep_size = lax.axis_size("ep")
    me = lax.axis_index("ep")
    local_experts = gate_up.shape[0]
    hidden_width = down.shape[1]
    slice_width = out_weight.shape[0]
    group_rows = row_count * ep_size
    ring = ring_order(ep_size)
    pos = jnp.array([ring.index(p) for p in range(ep_size)], dtype=jnp.int32)[me]

    with jax.named_scope("route_weights"):
        expert_ids = jnp.arange(local_experts * ep_size, dtype=jnp.int32)
        dense_weight = jnp.sum(
            jnp.where(route_ids[:, :, None] == expert_ids, route_weight[:, :, None], 0.0), axis=1
        )
        dense_weight = dense_weight.reshape(row_count, ep_size, local_experts).transpose(1, 0, 2)
        row_weights = lax.all_to_all(dense_weight, "ep", split_axis=0, concat_axis=0, tiled=True)
        row_weights = row_weights.reshape(group_rows, local_experts)

    with jax.named_scope("out_projection"):
        columns = attn_out.reshape(row_count, ep_size, slice_width).transpose(1, 0, 2)
        columns = lax.all_to_all(columns, "ep", split_axis=0, concat_axis=0, tiled=True)
        columns, row_weights = lax.optimization_barrier((columns, row_weights))
        partial = jnp.dot(
            columns.reshape(group_rows, slice_width), out_weight, preferred_element_type=jnp.float32
        )
        projected = ring_reduce_scatter(partial.reshape(ep_size, row_count, model_width), ring, pos)
        middle = (residual.astype(jnp.float32) + projected).astype(jnp.bfloat16)

    normed = rms_scale(middle.astype(jnp.float32), post_gain).astype(jnp.bfloat16)
    with jax.named_scope("dispatch_gather"):
        arrived = ring_all_gather(normed, ring, pos)

    ring_index = jnp.array(ring, dtype=jnp.int32)
    weight_blocks = row_weights.reshape(ep_size, row_count, local_experts)
    half = row_count // 2

    def step_weights(step):
        owner_fwd = ring_index[(pos - 1 - step) % ep_size]
        owner_bwd = ring_index[(pos + 1 + step) % ep_size]
        w_fwd = lax.dynamic_index_in_dim(weight_blocks, owner_fwd, 0, keepdims=False)[:half]
        w_bwd = lax.dynamic_index_in_dim(weight_blocks, owner_bwd, 0, keepdims=False)[half:]
        return w_fwd, w_bwd

    with jax.named_scope("local_experts"):
        steps_all = list(range(ep_size - 1))
        chunks = [[step] for step in steps_all]
        pieces = [None] * (ep_size - 1)
        own_part = None
        for c, steps in enumerate(chunks):
            rows_in = []
            weights_in = []
            for step in steps:
                rows_in += list(arrived[step])
                weights_in += list(step_weights(step))
            if c == len(chunks) - 1:
                rows_in.append(normed)
                weights_in.append(lax.dynamic_index_in_dim(weight_blocks, me, 0, keepdims=False))
            mixed = expert_mix(
                jnp.concatenate(rows_in, axis=0), jnp.concatenate(weights_in, axis=0), gate_up, down
            )
            for i, step in enumerate(steps):
                pieces[step] = (mixed[(2 * i) * half : (2 * i + 1) * half],
                                mixed[(2 * i + 1) * half : (2 * i + 2) * half])
            if c == len(chunks) - 1:
                own_part = mixed[2 * len(steps) * half :]

    with jax.named_scope("combine_return"):
        combined = ring_reduce_scatter_steps(pieces, own_part, ring)
    updated = middle.astype(jnp.float32) + combined
    return (updated.astype(jnp.bfloat16), rms_scale(updated, final_gain).astype(jnp.bfloat16))


def solution(mesh):
    in_specs = (
        P(("rep", "ep"), None),
        P(("rep", "ep"), None),
        P("ep", None),
        P(),
        P("ep", None, None),
        P("ep", None, None),
        P(("rep", "ep"), None),
        P(("rep", "ep"), None),
        P(),
    )
    out_specs = (P(("rep", "ep"), None), P(("rep", "ep"), None))
    return jax.shard_map(body, mesh=mesh, in_specs=in_specs, out_specs=out_specs, check_vma=False)
```

```python
import jax
import jax.numpy as jnp
from jax import lax
from jax.sharding import PartitionSpec as P


def rms_scale(values, scale_gain):
    mean_square = jnp.mean(values * values, axis=-1, keepdims=True)
    return values * lax.rsqrt(mean_square + 1e-06) * scale_gain


def ring_order(n):
    if n % 2:
        return list(range(n))
    return list(range(0, n, 2)) + list(range(n - 1, 0, -2))


def ring_reduce_scatter(blocks, ring, pos):
    n, rows, _ = blocks.shape
    half = rows // 2
    ring_index = jnp.array(ring, dtype=jnp.int32)
    forward = [(ring[q], ring[(q + 1) % n]) for q in range(n)]
    backward = [(ring[q], ring[(q - 1) % n]) for q in range(n)]
    got_fwd = got_bwd = None
    for step in range(n - 1):
        owner_fwd = ring_index[(pos - 1 - step) % n]
        owner_bwd = ring_index[(pos + 1 + step) % n]
        send_fwd = lax.dynamic_index_in_dim(blocks, owner_fwd, 0, keepdims=False)[:half]
        send_bwd = lax.dynamic_index_in_dim(blocks, owner_bwd, 0, keepdims=False)[half:]
        if step:
            send_fwd = send_fwd + got_fwd
            send_bwd = send_bwd + got_bwd
        send_fwd, send_bwd = lax.optimization_barrier(
            (send_fwd.astype(jnp.bfloat16), send_bwd.astype(jnp.bfloat16))
        )
        got_fwd, got_bwd = lax.optimization_barrier(
            (lax.ppermute(send_fwd, "ep", forward), lax.ppermute(send_bwd, "ep", backward))
        )
        got_fwd = got_fwd.astype(jnp.float32)
        got_bwd = got_bwd.astype(jnp.float32)
    me = ring_index[pos]
    own = lax.dynamic_index_in_dim(blocks, me, 0, keepdims=False)
    return jnp.concatenate([own[:half] + got_fwd, own[half:] + got_bwd], axis=0)


def ring_all_gather(block, ring, pos):
    n = len(ring)
    half = block.shape[0] // 2
    forward = [(ring[q], ring[(q + 1) % n]) for q in range(n)]
    backward = [(ring[q], ring[(q - 1) % n]) for q in range(n)]
    got_fwd, got_bwd = block[:half], block[half:]
    arrived = []
    for step in range(n - 1):
        got_fwd, got_bwd = lax.optimization_barrier(
            (lax.ppermute(got_fwd, "ep", forward), lax.ppermute(got_bwd, "ep", backward))
        )
        arrived.append((got_fwd, got_bwd))
    return arrived


def ring_reduce_scatter_steps(pieces, own, ring):
    n = len(ring)
    forward = [(ring[q], ring[(q + 1) % n]) for q in range(n)]
    backward = [(ring[q], ring[(q - 1) % n]) for q in range(n)]
    got_fwd = got_bwd = None
    for step in range(n - 1):
        send_fwd, send_bwd = pieces[step]
        if step:
            send_fwd = send_fwd + got_fwd
            send_bwd = send_bwd + got_bwd
        send_fwd, send_bwd = lax.optimization_barrier(
            (send_fwd.astype(jnp.bfloat16), send_bwd.astype(jnp.bfloat16))
        )
        got_fwd, got_bwd = lax.optimization_barrier(
            (lax.ppermute(send_fwd, "ep", forward), lax.ppermute(send_bwd, "ep", backward))
        )
        got_fwd = got_fwd.astype(jnp.float32)
        got_bwd = got_bwd.astype(jnp.float32)
    half = own.shape[0] // 2
    return jnp.concatenate([own[:half] + got_fwd, own[half:] + got_bwd], axis=0)


def expert_mix(rows, weights, gate_up, down):
    hidden_width = down.shape[1]
    total = None
    for e in range(gate_up.shape[0]):
        projected_up = jnp.dot(rows, gate_up[e], preferred_element_type=jnp.float32)
        activated = (
            jax.nn.silu(projected_up[:, :hidden_width]) * projected_up[:, hidden_width:]
        ).astype(jnp.bfloat16)
        expert_out = jnp.dot(activated, down[e], preferred_element_type=jnp.float32).astype(
            jnp.bfloat16
        )
        term = weights[:, e : e + 1] * expert_out.astype(jnp.float32)
        total = term if total is None else total + term
    return total


def body(
    residual, attn_out, out_weight, post_gain, gate_up, down, route_ids, route_weight, final_gain
):
    row_count, model_width = residual.shape
    ep_size = lax.axis_size("ep")
    me = lax.axis_index("ep")
    local_experts = gate_up.shape[0]
    hidden_width = down.shape[1]
    slice_width = out_weight.shape[0]
    group_rows = row_count * ep_size
    ring = ring_order(ep_size)
    pos = jnp.array([ring.index(p) for p in range(ep_size)], dtype=jnp.int32)[me]

    with jax.named_scope("route_weights"):
        expert_ids = jnp.arange(local_experts * ep_size, dtype=jnp.int32)
        dense_weight = jnp.sum(
            jnp.where(route_ids[:, :, None] == expert_ids, route_weight[:, :, None], 0.0), axis=1
        )
        dense_weight = dense_weight.reshape(row_count, ep_size, local_experts).transpose(1, 0, 2)
        row_weights = lax.all_to_all(dense_weight, "ep", split_axis=0, concat_axis=0, tiled=True)
        row_weights = row_weights.reshape(group_rows, local_experts)

    with jax.named_scope("out_projection"):
        columns = attn_out.reshape(row_count, ep_size, slice_width).transpose(1, 0, 2)
        columns = lax.all_to_all(columns, "ep", split_axis=0, concat_axis=0, tiled=True)
        columns, row_weights = lax.optimization_barrier((columns, row_weights))
        partial = jnp.dot(
            columns.reshape(group_rows, slice_width), out_weight, preferred_element_type=jnp.float32
        )
        projected = ring_reduce_scatter(partial.reshape(ep_size, row_count, model_width), ring, pos)
        middle = (residual.astype(jnp.float32) + projected).astype(jnp.bfloat16)

    normed = rms_scale(middle.astype(jnp.float32), post_gain).astype(jnp.bfloat16)
    with jax.named_scope("dispatch_gather"):
        arrived = ring_all_gather(normed, ring, pos)

    ring_index = jnp.array(ring, dtype=jnp.int32)
    weight_blocks = row_weights.reshape(ep_size, row_count, local_experts)
    half = row_count // 2

    def step_weights(step):
        owner_fwd = ring_index[(pos - 1 - step) % ep_size]
        owner_bwd = ring_index[(pos + 1 + step) % ep_size]
        w_fwd = lax.dynamic_index_in_dim(weight_blocks, owner_fwd, 0, keepdims=False)[:half]
        w_bwd = lax.dynamic_index_in_dim(weight_blocks, owner_bwd, 0, keepdims=False)[half:]
        return w_fwd, w_bwd

    with jax.named_scope("local_experts"):
        steps_all = list(range(ep_size - 1))
        chunks = [steps_all[:1]] + [steps_all[i : i + 2] for i in range(1, ep_size - 1, 2)]
        pieces = [None] * (ep_size - 1)
        own_part = None
        for c, steps in enumerate(chunks):
            rows_in = []
            weights_in = []
            for step in steps:
                rows_in += list(arrived[step])
                weights_in += list(step_weights(step))
            if c == len(chunks) - 1:
                rows_in.append(normed)
                weights_in.append(lax.dynamic_index_in_dim(weight_blocks, me, 0, keepdims=False))
            mixed = expert_mix(
                jnp.concatenate(rows_in, axis=0), jnp.concatenate(weights_in, axis=0), gate_up, down
            )
            for i, step in enumerate(steps):
                pieces[step] = (mixed[(2 * i) * half : (2 * i + 1) * half],
                                mixed[(2 * i + 1) * half : (2 * i + 2) * half])
            if c == len(chunks) - 1:
                own_part = mixed[2 * len(steps) * half :]

    with jax.named_scope("combine_return"):
        combined = ring_reduce_scatter_steps(pieces, own_part, ring)
    updated = middle.astype(jnp.float32) + combined
    return (updated.astype(jnp.bfloat16), rms_scale(updated, final_gain).astype(jnp.bfloat16))


def solution(mesh):
    in_specs = (
        P(("rep", "ep"), None),
        P(("rep", "ep"), None),
        P("ep", None),
        P(),
        P("ep", None, None),
        P("ep", None, None),
        P(("rep", "ep"), None),
        P(("rep", "ep"), None),
        P(),
    )
    out_specs = (P(("rep", "ep"), None), P(("rep", "ep"), None))
    return jax.shard_map(body, mesh=mesh, in_specs=in_specs, out_specs=out_specs, check_vma=False)
```

```python
import jax
import jax.numpy as jnp
from jax import lax
from jax.sharding import PartitionSpec as P


def rms_scale(values, scale_gain):
    mean_square = jnp.mean(values * values, axis=-1, keepdims=True)
    return values * lax.rsqrt(mean_square + 1e-06) * scale_gain


def ring_order(n):
    if n % 2:
        return list(range(n))
    return list(range(0, n, 2)) + list(range(n - 1, 0, -2))


def ring_reduce_scatter(blocks, ring, pos):
    n, rows, _ = blocks.shape
    half = rows // 2
    ring_index = jnp.array(ring, dtype=jnp.int32)
    forward = [(ring[q], ring[(q + 1) % n]) for q in range(n)]
    backward = [(ring[q], ring[(q - 1) % n]) for q in range(n)]
    got_fwd = got_bwd = None
    for step in range(n - 1):
        owner_fwd = ring_index[(pos - 1 - step) % n]
        owner_bwd = ring_index[(pos + 1 + step) % n]
        send_fwd = lax.dynamic_index_in_dim(blocks, owner_fwd, 0, keepdims=False)[:half]
        send_bwd = lax.dynamic_index_in_dim(blocks, owner_bwd, 0, keepdims=False)[half:]
        if step:
            send_fwd = send_fwd + got_fwd
            send_bwd = send_bwd + got_bwd
        send_fwd, send_bwd = lax.optimization_barrier(
            (send_fwd.astype(jnp.bfloat16), send_bwd.astype(jnp.bfloat16))
        )
        got_fwd, got_bwd = lax.optimization_barrier(
            (lax.ppermute(send_fwd, "ep", forward), lax.ppermute(send_bwd, "ep", backward))
        )
        got_fwd = got_fwd.astype(jnp.float32)
        got_bwd = got_bwd.astype(jnp.float32)
    me = ring_index[pos]
    own = lax.dynamic_index_in_dim(blocks, me, 0, keepdims=False)
    return jnp.concatenate([own[:half] + got_fwd, own[half:] + got_bwd], axis=0)


def ring_all_gather(block, ring, pos):
    n = len(ring)
    half = block.shape[0] // 2
    forward = [(ring[q], ring[(q + 1) % n]) for q in range(n)]
    backward = [(ring[q], ring[(q - 1) % n]) for q in range(n)]
    got_fwd, got_bwd = block[:half], block[half:]
    arrived = []
    for step in range(n - 1):
        got_fwd, got_bwd = lax.optimization_barrier(
            (lax.ppermute(got_fwd, "ep", forward), lax.ppermute(got_bwd, "ep", backward))
        )
        arrived.append((got_fwd, got_bwd))
    return arrived


def ring_reduce_scatter_steps(pieces, own, ring):
    n = len(ring)
    forward = [(ring[q], ring[(q + 1) % n]) for q in range(n)]
    backward = [(ring[q], ring[(q - 1) % n]) for q in range(n)]
    got_fwd = got_bwd = None
    for step in range(n - 1):
        send_fwd, send_bwd = pieces[step]
        if step:
            send_fwd = send_fwd + got_fwd
            send_bwd = send_bwd + got_bwd
        send_fwd, send_bwd = lax.optimization_barrier(
            (send_fwd.astype(jnp.bfloat16), send_bwd.astype(jnp.bfloat16))
        )
        got_fwd, got_bwd = lax.optimization_barrier(
            (lax.ppermute(send_fwd, "ep", forward), lax.ppermute(send_bwd, "ep", backward))
        )
        got_fwd = got_fwd.astype(jnp.float32)
        got_bwd = got_bwd.astype(jnp.float32)
    half = own.shape[0] // 2
    return jnp.concatenate([own[:half] + got_fwd, own[half:] + got_bwd], axis=0)


def expert_mix(rows, weights, gate_up, down):
    hidden_width = down.shape[1]
    total = None
    for e in range(gate_up.shape[0]):
        projected_up = jnp.dot(rows, gate_up[e], preferred_element_type=jnp.float32)
        activated = (
            jax.nn.silu(projected_up[:, :hidden_width]) * projected_up[:, hidden_width:]
        ).astype(jnp.bfloat16)
        expert_out = jnp.dot(activated, down[e], preferred_element_type=jnp.float32).astype(
            jnp.bfloat16
        )
        term = weights[:, e : e + 1] * expert_out.astype(jnp.float32)
        total = term if total is None else total + term
    return total


def body(
    residual, attn_out, out_weight, post_gain, gate_up, down, route_ids, route_weight, final_gain
):
    row_count, model_width = residual.shape
    ep_size = lax.axis_size("ep")
    me = lax.axis_index("ep")
    local_experts = gate_up.shape[0]
    hidden_width = down.shape[1]
    slice_width = out_weight.shape[0]
    group_rows = row_count * ep_size
    ring = ring_order(ep_size)
    pos = jnp.array([ring.index(p) for p in range(ep_size)], dtype=jnp.int32)[me]

    with jax.named_scope("route_weights"):
        expert_ids = jnp.arange(local_experts * ep_size, dtype=jnp.int32)
        dense_weight = jnp.sum(
            jnp.where(route_ids[:, :, None] == expert_ids, route_weight[:, :, None], 0.0), axis=1
        )
        dense_weight = dense_weight.reshape(row_count, ep_size, local_experts).transpose(1, 0, 2)
        row_weights = lax.all_to_all(dense_weight, "ep", split_axis=0, concat_axis=0, tiled=True)
        row_weights = row_weights.reshape(group_rows, local_experts)

    with jax.named_scope("out_projection"):
        columns = attn_out.reshape(row_count, ep_size, slice_width).transpose(1, 0, 2)
        columns = lax.all_to_all(columns, "ep", split_axis=0, concat_axis=0, tiled=True)
        columns, row_weights = lax.optimization_barrier((columns, row_weights))
        ring_index = jnp.array(ring, dtype=jnp.int32)
        half = row_count // 2
        pieces = []
        for step in range(ep_size - 1):
            owner_fwd = ring_index[(pos - 1 - step) % ep_size]
            owner_bwd = ring_index[(pos + 1 + step) % ep_size]
            rows_in = jnp.concatenate(
                [
                    lax.dynamic_index_in_dim(columns, owner_fwd, 0, keepdims=False)[:half],
                    lax.dynamic_index_in_dim(columns, owner_bwd, 0, keepdims=False)[half:],
                ],
                axis=0,
            )
            part = jnp.dot(rows_in, out_weight, preferred_element_type=jnp.float32)
            pieces.append((part[:half], part[half:]))
        own_part = jnp.dot(
            lax.dynamic_index_in_dim(columns, me, 0, keepdims=False),
            out_weight,
            preferred_element_type=jnp.float32,
        )
        projected = ring_reduce_scatter_steps(pieces, own_part, ring)
        middle = (residual.astype(jnp.float32) + projected).astype(jnp.bfloat16)

    normed = rms_scale(middle.astype(jnp.float32), post_gain).astype(jnp.bfloat16)
    with jax.named_scope("dispatch_gather"):
        arrived = ring_all_gather(normed, ring, pos)

    ring_index = jnp.array(ring, dtype=jnp.int32)
    weight_blocks = row_weights.reshape(ep_size, row_count, local_experts)
    half = row_count // 2

    def step_weights(step):
        owner_fwd = ring_index[(pos - 1 - step) % ep_size]
        owner_bwd = ring_index[(pos + 1 + step) % ep_size]
        w_fwd = lax.dynamic_index_in_dim(weight_blocks, owner_fwd, 0, keepdims=False)[:half]
        w_bwd = lax.dynamic_index_in_dim(weight_blocks, owner_bwd, 0, keepdims=False)[half:]
        return w_fwd, w_bwd

    with jax.named_scope("local_experts"):
        steps_all = list(range(ep_size - 1))
        chunks = [steps_all[i : i + 2] for i in range(0, ep_size - 1, 2)]
        pieces = [None] * (ep_size - 1)
        own_part = None
        for c, steps in enumerate(chunks):
            rows_in = []
            weights_in = []
            for step in steps:
                rows_in += list(arrived[step])
                weights_in += list(step_weights(step))
            if c == len(chunks) - 1:
                rows_in.append(normed)
                weights_in.append(lax.dynamic_index_in_dim(weight_blocks, me, 0, keepdims=False))
            mixed = expert_mix(
                jnp.concatenate(rows_in, axis=0), jnp.concatenate(weights_in, axis=0), gate_up, down
            )
            for i, step in enumerate(steps):
                pieces[step] = (mixed[(2 * i) * half : (2 * i + 1) * half],
                                mixed[(2 * i + 1) * half : (2 * i + 2) * half])
            if c == len(chunks) - 1:
                own_part = mixed[2 * len(steps) * half :]

    with jax.named_scope("combine_return"):
        combined = ring_reduce_scatter_steps(pieces, own_part, ring)
    updated = middle.astype(jnp.float32) + combined
    return (updated.astype(jnp.bfloat16), rms_scale(updated, final_gain).astype(jnp.bfloat16))


def solution(mesh):
    in_specs = (
        P(("rep", "ep"), None),
        P(("rep", "ep"), None),
        P("ep", None),
        P(),
        P("ep", None, None),
        P("ep", None, None),
        P(("rep", "ep"), None),
        P(("rep", "ep"), None),
        P(),
    )
    out_specs = (P(("rep", "ep"), None), P(("rep", "ep"), None))
    return jax.shard_map(body, mesh=mesh, in_specs=in_specs, out_specs=out_specs, check_vma=False)
```

```python
import jax
import jax.numpy as jnp
from jax import lax
from jax.sharding import PartitionSpec as P


def rms_scale(values, scale_gain):
    mean_square = jnp.mean(values * values, axis=-1, keepdims=True)
    return values * lax.rsqrt(mean_square + 1e-06) * scale_gain


def ring_order(n):
    if n % 2:
        return list(range(n))
    return list(range(0, n, 2)) + list(range(n - 1, 0, -2))


def ring_reduce_scatter(blocks, ring, pos):
    n, rows, _ = blocks.shape
    half = rows // 2
    ring_index = jnp.array(ring, dtype=jnp.int32)
    forward = [(ring[q], ring[(q + 1) % n]) for q in range(n)]
    backward = [(ring[q], ring[(q - 1) % n]) for q in range(n)]
    got_fwd = got_bwd = None
    for step in range(n - 1):
        owner_fwd = ring_index[(pos - 1 - step) % n]
        owner_bwd = ring_index[(pos + 1 + step) % n]
        send_fwd = lax.dynamic_index_in_dim(blocks, owner_fwd, 0, keepdims=False)[:half]
        send_bwd = lax.dynamic_index_in_dim(blocks, owner_bwd, 0, keepdims=False)[half:]
        if step:
            send_fwd = send_fwd + got_fwd
            send_bwd = send_bwd + got_bwd
        send_fwd, send_bwd = lax.optimization_barrier(
            (send_fwd.astype(jnp.bfloat16), send_bwd.astype(jnp.bfloat16))
        )
        got_fwd, got_bwd = lax.optimization_barrier(
            (lax.ppermute(send_fwd, "ep", forward), lax.ppermute(send_bwd, "ep", backward))
        )
        got_fwd = got_fwd.astype(jnp.float32)
        got_bwd = got_bwd.astype(jnp.float32)
    me = ring_index[pos]
    own = lax.dynamic_index_in_dim(blocks, me, 0, keepdims=False)
    return jnp.concatenate([own[:half] + got_fwd, own[half:] + got_bwd], axis=0)


def ring_all_gather(block, ring, pos):
    n = len(ring)
    half = block.shape[0] // 2
    forward = [(ring[q], ring[(q + 1) % n]) for q in range(n)]
    backward = [(ring[q], ring[(q - 1) % n]) for q in range(n)]
    got_fwd, got_bwd = block[:half], block[half:]
    arrived = []
    for step in range(n - 1):
        got_fwd, got_bwd = lax.optimization_barrier(
            (lax.ppermute(got_fwd, "ep", forward), lax.ppermute(got_bwd, "ep", backward))
        )
        arrived.append((got_fwd, got_bwd))
    return arrived


def ring_reduce_scatter_steps(pieces, own, ring):
    n = len(ring)
    forward = [(ring[q], ring[(q + 1) % n]) for q in range(n)]
    backward = [(ring[q], ring[(q - 1) % n]) for q in range(n)]
    got_fwd = got_bwd = None
    for step in range(n - 1):
        send_fwd, send_bwd = pieces[step]
        if step:
            send_fwd = send_fwd + got_fwd
            send_bwd = send_bwd + got_bwd
        send_fwd, send_bwd = lax.optimization_barrier(
            (send_fwd.astype(jnp.bfloat16), send_bwd.astype(jnp.bfloat16))
        )
        got_fwd, got_bwd = lax.optimization_barrier(
            (lax.ppermute(send_fwd, "ep", forward), lax.ppermute(send_bwd, "ep", backward))
        )
        got_fwd = got_fwd.astype(jnp.float32)
        got_bwd = got_bwd.astype(jnp.float32)
    half = own.shape[0] // 2
    return jnp.concatenate([own[:half] + got_fwd, own[half:] + got_bwd], axis=0)


def expert_mix(rows, weights, gate_up, down):
    hidden_width = down.shape[1]
    total = None
    for e in range(gate_up.shape[0]):
        projected_up = jnp.dot(rows, gate_up[e], preferred_element_type=jnp.float32)
        activated = (
            jax.nn.silu(projected_up[:, :hidden_width]) * projected_up[:, hidden_width:]
        ).astype(jnp.bfloat16)
        expert_out = jnp.dot(activated, down[e], preferred_element_type=jnp.float32).astype(
            jnp.bfloat16
        )
        term = weights[:, e : e + 1] * expert_out.astype(jnp.float32)
        total = term if total is None else total + term
    return total


def body(
    residual, attn_out, out_weight, post_gain, gate_up, down, route_ids, route_weight, final_gain
):
    row_count, model_width = residual.shape
    ep_size = lax.axis_size("ep")
    me = lax.axis_index("ep")
    local_experts = gate_up.shape[0]
    hidden_width = down.shape[1]
    slice_width = out_weight.shape[0]
    group_rows = row_count * ep_size
    ring = ring_order(ep_size)
    pos = jnp.array([ring.index(p) for p in range(ep_size)], dtype=jnp.int32)[me]

    with jax.named_scope("route_weights"):
        expert_ids = jnp.arange(local_experts * ep_size, dtype=jnp.int32)
        dense_weight = jnp.sum(
            jnp.where(route_ids[:, :, None] == expert_ids, route_weight[:, :, None], 0.0), axis=1
        )
        dense_weight = dense_weight.reshape(row_count, ep_size, local_experts).transpose(1, 0, 2)
        row_weights = lax.all_to_all(dense_weight, "ep", split_axis=0, concat_axis=0, tiled=True)
        row_weights = row_weights.reshape(group_rows, local_experts)

    with jax.named_scope("out_projection"):
        columns = attn_out.reshape(row_count, ep_size, slice_width).transpose(1, 0, 2)
        columns = lax.all_to_all(columns, "ep", split_axis=0, concat_axis=0, tiled=True)
        columns, row_weights = lax.optimization_barrier((columns, row_weights))
        partial = jnp.dot(
            columns.reshape(group_rows, slice_width), out_weight, preferred_element_type=jnp.float32
        )
        projected = ring_reduce_scatter(partial.reshape(ep_size, row_count, model_width), ring, pos)
        middle = (residual.astype(jnp.float32) + projected).astype(jnp.bfloat16)

    normed = rms_scale(middle.astype(jnp.float32), post_gain).astype(jnp.bfloat16)
    with jax.named_scope("dispatch_gather"):
        arrived = ring_all_gather(normed, ring, pos)

    ring_index = jnp.array(ring, dtype=jnp.int32)
    weight_blocks = row_weights.reshape(ep_size, row_count, local_experts)
    half = row_count // 2

    def step_weights(step):
        owner_fwd = ring_index[(pos - 1 - step) % ep_size]
        owner_bwd = ring_index[(pos + 1 + step) % ep_size]
        w_fwd = lax.dynamic_index_in_dim(weight_blocks, owner_fwd, 0, keepdims=False)[:half]
        w_bwd = lax.dynamic_index_in_dim(weight_blocks, owner_bwd, 0, keepdims=False)[half:]
        return w_fwd, w_bwd

    with jax.named_scope("local_experts"):
        steps_all = list(range(ep_size - 1))
        chunks = [steps_all[i : i + 2] for i in range(0, ep_size - 1, 2)]
        pieces = [None] * (ep_size - 1)
        own_part = None
        for c, steps in enumerate(chunks):
            rows_in = []
            weights_in = []
            for step in steps:
                rows_in += list(arrived[step])
                weights_in += list(step_weights(step))
            mixed = expert_mix(
                jnp.concatenate(rows_in, axis=0), jnp.concatenate(weights_in, axis=0), gate_up, down
            )
            for i, step in enumerate(steps):
                pieces[step] = (mixed[(2 * i) * half : (2 * i + 1) * half],
                                mixed[(2 * i + 1) * half : (2 * i + 2) * half])
        own_part = expert_mix(
            normed, lax.dynamic_index_in_dim(weight_blocks, me, 0, keepdims=False), gate_up, down
        )

    with jax.named_scope("combine_return"):
        combined = ring_reduce_scatter_steps(pieces, own_part, ring)
    updated = middle.astype(jnp.float32) + combined
    return (updated.astype(jnp.bfloat16), rms_scale(updated, final_gain).astype(jnp.bfloat16))


def solution(mesh):
    in_specs = (
        P(("rep", "ep"), None),
        P(("rep", "ep"), None),
        P("ep", None),
        P(),
        P("ep", None, None),
        P("ep", None, None),
        P(("rep", "ep"), None),
        P(("rep", "ep"), None),
        P(),
    )
    out_specs = (P(("rep", "ep"), None), P(("rep", "ep"), None))
    return jax.shard_map(body, mesh=mesh, in_specs=in_specs, out_specs=out_specs, check_vma=False)
```

```python
import jax
import jax.numpy as jnp
from jax import lax
from jax.sharding import PartitionSpec as P


def rms_scale(values, scale_gain):
    mean_square = jnp.mean(values * values, axis=-1, keepdims=True)
    return values * lax.rsqrt(mean_square + 1e-06) * scale_gain


def ring_order(n):
    if n % 2:
        return list(range(n))
    return list(range(0, n, 2)) + list(range(n - 1, 0, -2))


def ring_reduce_scatter(blocks, ring, pos):
    n, rows, _ = blocks.shape
    half = rows // 2
    ring_index = jnp.array(ring, dtype=jnp.int32)
    forward = [(ring[q], ring[(q + 1) % n]) for q in range(n)]
    backward = [(ring[q], ring[(q - 1) % n]) for q in range(n)]
    got_fwd = got_bwd = None
    for step in range(n - 1):
        owner_fwd = ring_index[(pos - 1 - step) % n]
        owner_bwd = ring_index[(pos + 1 + step) % n]
        send_fwd = lax.dynamic_index_in_dim(blocks, owner_fwd, 0, keepdims=False)[:half]
        send_bwd = lax.dynamic_index_in_dim(blocks, owner_bwd, 0, keepdims=False)[half:]
        send_fwd = send_fwd.astype(jnp.float32)
        send_bwd = send_bwd.astype(jnp.float32)
        if step:
            send_fwd = send_fwd + got_fwd
            send_bwd = send_bwd + got_bwd
        send_fwd, send_bwd = lax.optimization_barrier(
            (send_fwd.astype(jnp.bfloat16), send_bwd.astype(jnp.bfloat16))
        )
        got_fwd, got_bwd = lax.optimization_barrier(
            (lax.ppermute(send_fwd, "ep", forward), lax.ppermute(send_bwd, "ep", backward))
        )
        got_fwd = got_fwd.astype(jnp.float32)
        got_bwd = got_bwd.astype(jnp.float32)
    me = ring_index[pos]
    own = lax.dynamic_index_in_dim(blocks, me, 0, keepdims=False).astype(jnp.float32)
    return jnp.concatenate([own[:half] + got_fwd, own[half:] + got_bwd], axis=0)


def ring_all_gather(block, ring, pos):
    n = len(ring)
    half = block.shape[0] // 2
    forward = [(ring[q], ring[(q + 1) % n]) for q in range(n)]
    backward = [(ring[q], ring[(q - 1) % n]) for q in range(n)]
    got_fwd, got_bwd = block[:half], block[half:]
    arrived = []
    for step in range(n - 1):
        got_fwd, got_bwd = lax.optimization_barrier(
            (lax.ppermute(got_fwd, "ep", forward), lax.ppermute(got_bwd, "ep", backward))
        )
        arrived.append((got_fwd, got_bwd))
    return arrived


def ring_reduce_scatter_steps(pieces, own, ring):
    n = len(ring)
    forward = [(ring[q], ring[(q + 1) % n]) for q in range(n)]
    backward = [(ring[q], ring[(q - 1) % n]) for q in range(n)]
    got_fwd = got_bwd = None
    for step in range(n - 1):
        send_fwd, send_bwd = pieces[step]
        if step:
            send_fwd = send_fwd + got_fwd
            send_bwd = send_bwd + got_bwd
        send_fwd, send_bwd = lax.optimization_barrier(
            (send_fwd.astype(jnp.bfloat16), send_bwd.astype(jnp.bfloat16))
        )
        got_fwd, got_bwd = lax.optimization_barrier(
            (lax.ppermute(send_fwd, "ep", forward), lax.ppermute(send_bwd, "ep", backward))
        )
        got_fwd = got_fwd.astype(jnp.float32)
        got_bwd = got_bwd.astype(jnp.float32)
    half = own.shape[0] // 2
    return jnp.concatenate([own[:half] + got_fwd, own[half:] + got_bwd], axis=0)


def expert_mix(rows, weights, gate_up, down):
    hidden_width = down.shape[1]
    total = None
    for e in range(gate_up.shape[0]):
        projected_up = jnp.dot(rows, gate_up[e], preferred_element_type=jnp.float32)
        activated = (
            jax.nn.silu(projected_up[:, :hidden_width]) * projected_up[:, hidden_width:]
        ).astype(jnp.bfloat16)
        expert_out = jnp.dot(activated, down[e], preferred_element_type=jnp.float32).astype(
            jnp.bfloat16
        )
        term = weights[:, e : e + 1] * expert_out.astype(jnp.float32)
        total = term if total is None else total + term
    return total


def body(
    residual, attn_out, out_weight, post_gain, gate_up, down, route_ids, route_weight, final_gain
):
    row_count, model_width = residual.shape
    ep_size = lax.axis_size("ep")
    me = lax.axis_index("ep")
    local_experts = gate_up.shape[0]
    hidden_width = down.shape[1]
    slice_width = out_weight.shape[0]
    group_rows = row_count * ep_size
    ring = ring_order(ep_size)
    pos = jnp.array([ring.index(p) for p in range(ep_size)], dtype=jnp.int32)[me]

    with jax.named_scope("route_weights"):
        expert_ids = jnp.arange(local_experts * ep_size, dtype=jnp.int32)
        dense_weight = jnp.sum(
            jnp.where(route_ids[:, :, None] == expert_ids, route_weight[:, :, None], 0.0), axis=1
        )
        dense_weight = dense_weight.reshape(row_count, ep_size, local_experts).transpose(1, 0, 2)
        row_weights = lax.all_to_all(dense_weight, "ep", split_axis=0, concat_axis=0, tiled=True)
        row_weights = row_weights.reshape(group_rows, local_experts)

    with jax.named_scope("out_projection"):
        columns = attn_out.reshape(row_count, ep_size, slice_width).transpose(1, 0, 2)
        columns = lax.all_to_all(columns, "ep", split_axis=0, concat_axis=0, tiled=True)
        columns, row_weights = lax.optimization_barrier((columns, row_weights))
        partial = jnp.dot(
            columns.reshape(group_rows, slice_width), out_weight, preferred_element_type=jnp.float32
        ).astype(jnp.bfloat16)
        projected = ring_reduce_scatter(partial.reshape(ep_size, row_count, model_width), ring, pos)
        middle = (residual.astype(jnp.float32) + projected).astype(jnp.bfloat16)

    normed = rms_scale(middle.astype(jnp.float32), post_gain).astype(jnp.bfloat16)
    with jax.named_scope("dispatch_gather"):
        arrived = ring_all_gather(normed, ring, pos)

    ring_index = jnp.array(ring, dtype=jnp.int32)
    weight_blocks = row_weights.reshape(ep_size, row_count, local_experts)
    half = row_count // 2

    def step_weights(step):
        owner_fwd = ring_index[(pos - 1 - step) % ep_size]
        owner_bwd = ring_index[(pos + 1 + step) % ep_size]
        w_fwd = lax.dynamic_index_in_dim(weight_blocks, owner_fwd, 0, keepdims=False)[:half]
        w_bwd = lax.dynamic_index_in_dim(weight_blocks, owner_bwd, 0, keepdims=False)[half:]
        return w_fwd, w_bwd

    with jax.named_scope("local_experts"):
        steps_all = list(range(ep_size - 1))
        chunks = [steps_all[i : i + 2] for i in range(0, ep_size - 1, 2)]
        pieces = [None] * (ep_size - 1)
        own_part = None
        for c, steps in enumerate(chunks):
            rows_in = []
            weights_in = []
            for step in steps:
                rows_in += list(arrived[step])
                weights_in += list(step_weights(step))
            if c == len(chunks) - 1:
                rows_in.append(normed)
                weights_in.append(lax.dynamic_index_in_dim(weight_blocks, me, 0, keepdims=False))
            mixed = expert_mix(
                jnp.concatenate(rows_in, axis=0), jnp.concatenate(weights_in, axis=0), gate_up, down
            )
            for i, step in enumerate(steps):
                pieces[step] = (mixed[(2 * i) * half : (2 * i + 1) * half],
                                mixed[(2 * i + 1) * half : (2 * i + 2) * half])
            if c == len(chunks) - 1:
                own_part = mixed[2 * len(steps) * half :]

    with jax.named_scope("combine_return"):
        combined = ring_reduce_scatter_steps(pieces, own_part, ring)
    updated = middle.astype(jnp.float32) + combined
    return (updated.astype(jnp.bfloat16), rms_scale(updated, final_gain).astype(jnp.bfloat16))


def solution(mesh):
    in_specs = (
        P(("rep", "ep"), None),
        P(("rep", "ep"), None),
        P("ep", None),
        P(),
        P("ep", None, None),
        P("ep", None, None),
        P(("rep", "ep"), None),
        P(("rep", "ep"), None),
        P(),
    )
    out_specs = (P(("rep", "ep"), None), P(("rep", "ep"), None))
    return jax.shard_map(body, mesh=mesh, in_specs=in_specs, out_specs=out_specs, check_vma=False)
```

```python
import jax
import jax.numpy as jnp
from jax import lax
from jax.sharding import PartitionSpec as P


def rms_scale(values, scale_gain):
    mean_square = jnp.mean(values * values, axis=-1, keepdims=True)
    return values * lax.rsqrt(mean_square + 1e-06) * scale_gain


def ring_order(n):
    if n % 2:
        return list(range(n))
    return list(range(0, n, 2)) + list(range(n - 1, 0, -2))


def ring_reduce_scatter(blocks, ring, pos):
    n, rows, _ = blocks.shape
    half = rows // 2
    ring_index = jnp.array(ring, dtype=jnp.int32)
    forward = [(ring[q], ring[(q + 1) % n]) for q in range(n)]
    backward = [(ring[q], ring[(q - 1) % n]) for q in range(n)]
    got_fwd = got_bwd = None
    for step in range(n - 1):
        owner_fwd = ring_index[(pos - 1 - step) % n]
        owner_bwd = ring_index[(pos + 1 + step) % n]
        send_fwd = lax.dynamic_index_in_dim(blocks, owner_fwd, 0, keepdims=False)[:half]
        send_bwd = lax.dynamic_index_in_dim(blocks, owner_bwd, 0, keepdims=False)[half:]
        if step:
            send_fwd = send_fwd + got_fwd
            send_bwd = send_bwd + got_bwd
        send_fwd, send_bwd = lax.optimization_barrier(
            (send_fwd.astype(jnp.bfloat16), send_bwd.astype(jnp.bfloat16))
        )
        got_fwd, got_bwd = lax.optimization_barrier(
            (lax.ppermute(send_fwd, "ep", forward), lax.ppermute(send_bwd, "ep", backward))
        )
        got_fwd = got_fwd.astype(jnp.float32)
        got_bwd = got_bwd.astype(jnp.float32)
    me = ring_index[pos]
    own = lax.dynamic_index_in_dim(blocks, me, 0, keepdims=False)
    return jnp.concatenate([own[:half] + got_fwd, own[half:] + got_bwd], axis=0)


def ring_all_gather(block, ring, pos):
    n = len(ring)
    half = block.shape[0] // 2
    forward = [(ring[q], ring[(q + 1) % n]) for q in range(n)]
    backward = [(ring[q], ring[(q - 1) % n]) for q in range(n)]
    got_fwd, got_bwd = block[:half], block[half:]
    arrived = []
    for step in range(n - 1):
        got_fwd, got_bwd = lax.optimization_barrier(
            (lax.ppermute(got_fwd, "ep", forward), lax.ppermute(got_bwd, "ep", backward))
        )
        arrived.append((got_fwd, got_bwd))
    return arrived


def ring_reduce_scatter_steps(pieces, own, ring):
    n = len(ring)
    forward = [(ring[q], ring[(q + 1) % n]) for q in range(n)]
    backward = [(ring[q], ring[(q - 1) % n]) for q in range(n)]
    got_fwd = got_bwd = None
    for step in range(n - 1):
        send_fwd, send_bwd = pieces[step]
        if step:
            send_fwd = send_fwd + got_fwd
            send_bwd = send_bwd + got_bwd
        send_fwd, send_bwd = lax.optimization_barrier(
            (send_fwd.astype(jnp.bfloat16), send_bwd.astype(jnp.bfloat16))
        )
        got_fwd, got_bwd = lax.optimization_barrier(
            (lax.ppermute(send_fwd, "ep", forward), lax.ppermute(send_bwd, "ep", backward))
        )
        got_fwd = got_fwd.astype(jnp.float32)
        got_bwd = got_bwd.astype(jnp.float32)
    half = own.shape[0] // 2
    return jnp.concatenate([own[:half] + got_fwd, own[half:] + got_bwd], axis=0)


def expert_mix(rows, weights, gate_up, down):
    hidden_width = down.shape[1]
    total = None
    for e in range(gate_up.shape[0]):
        projected_up = jnp.dot(rows, gate_up[e], preferred_element_type=jnp.float32)
        activated = (
            jax.nn.silu(projected_up[:, :hidden_width]) * projected_up[:, hidden_width:]
        ).astype(jnp.bfloat16)
        expert_out = jnp.dot(activated, down[e], preferred_element_type=jnp.float32).astype(
            jnp.bfloat16
        )
        term = weights[:, e : e + 1] * expert_out.astype(jnp.float32)
        total = term if total is None else total + term
    return total


def body(
    residual, attn_out, out_weight, post_gain, gate_up, down, route_ids, route_weight, final_gain
):
    row_count, model_width = residual.shape
    ep_size = lax.axis_size("ep")
    me = lax.axis_index("ep")
    local_experts = gate_up.shape[0]
    hidden_width = down.shape[1]
    slice_width = out_weight.shape[0]
    group_rows = row_count * ep_size
    ring = ring_order(ep_size)
    pos = jnp.array([ring.index(p) for p in range(ep_size)], dtype=jnp.int32)[me]

    with jax.named_scope("route_weights"):
        expert_ids = jnp.arange(local_experts * ep_size, dtype=jnp.int32)
        dense_weight = jnp.sum(
            jnp.where(route_ids[:, :, None] == expert_ids, route_weight[:, :, None], 0.0), axis=1
        )
        dense_weight = dense_weight.reshape(row_count, ep_size, local_experts).transpose(1, 0, 2)
        row_weights = lax.all_to_all(dense_weight, "ep", split_axis=0, concat_axis=0, tiled=True)
        row_weights = row_weights.reshape(group_rows, local_experts)

    with jax.named_scope("out_projection"):
        columns = attn_out.reshape(row_count, ep_size, slice_width).transpose(1, 0, 2)
        columns = lax.all_to_all(columns, "ep", split_axis=0, concat_axis=0, tiled=True)
        columns, row_weights = lax.optimization_barrier((columns, row_weights))
        partial = jnp.dot(
            columns.reshape(group_rows, slice_width), out_weight, preferred_element_type=jnp.float32
        )
        projected = ring_reduce_scatter(partial.reshape(ep_size, row_count, model_width), ring, pos)
        middle = (residual.astype(jnp.float32) + projected).astype(jnp.bfloat16)

    normed = rms_scale(middle.astype(jnp.float32), post_gain).astype(jnp.bfloat16)
    with jax.named_scope("dispatch_gather"):
        arrived = ring_all_gather(normed, ring, pos)

    ring_index = jnp.array(ring, dtype=jnp.int32)
    weight_blocks = row_weights.reshape(ep_size, row_count, local_experts)
    half = row_count // 2

    def step_weights(step):
        owner_fwd = ring_index[(pos - 1 - step) % ep_size]
        owner_bwd = ring_index[(pos + 1 + step) % ep_size]
        w_fwd = lax.dynamic_index_in_dim(weight_blocks, owner_fwd, 0, keepdims=False)[:half]
        w_bwd = lax.dynamic_index_in_dim(weight_blocks, owner_bwd, 0, keepdims=False)[half:]
        return w_fwd, w_bwd

    with jax.named_scope("local_experts"):
        steps_all = list(range(ep_size - 1))
        chunks = [steps_all[i : i + 2] for i in range(0, ep_size - 1, 2)]
        if len(chunks) > 2:
            chunks = chunks[:-2] + [chunks[-2] + chunks[-1]]
        pieces = [None] * (ep_size - 1)
        own_part = None
        for c, steps in enumerate(chunks):
            rows_in = []
            weights_in = []
            for step in steps:
                rows_in += list(arrived[step])
                weights_in += list(step_weights(step))
            if c == len(chunks) - 1:
                rows_in.append(normed)
                weights_in.append(lax.dynamic_index_in_dim(weight_blocks, me, 0, keepdims=False))
            mixed = expert_mix(
                jnp.concatenate(rows_in, axis=0), jnp.concatenate(weights_in, axis=0), gate_up, down
            )
            for i, step in enumerate(steps):
                pieces[step] = (mixed[(2 * i) * half : (2 * i + 1) * half],
                                mixed[(2 * i + 1) * half : (2 * i + 2) * half])
            if c == len(chunks) - 1:
                own_part = mixed[2 * len(steps) * half :]

    with jax.named_scope("combine_return"):
        combined = ring_reduce_scatter_steps(pieces, own_part, ring)
    updated = middle.astype(jnp.float32) + combined
    return (updated.astype(jnp.bfloat16), rms_scale(updated, final_gain).astype(jnp.bfloat16))


def solution(mesh):
    in_specs = (
        P(("rep", "ep"), None),
        P(("rep", "ep"), None),
        P("ep", None),
        P(),
        P("ep", None, None),
        P("ep", None, None),
        P(("rep", "ep"), None),
        P(("rep", "ep"), None),
        P(),
    )
    out_specs = (P(("rep", "ep"), None), P(("rep", "ep"), None))
    return jax.shard_map(body, mesh=mesh, in_specs=in_specs, out_specs=out_specs, check_vma=False)
```

```python
import jax
import jax.numpy as jnp
from jax import lax
from jax.sharding import PartitionSpec as P


def rms_scale(values, scale_gain):
    mean_square = jnp.mean(values * values, axis=-1, keepdims=True)
    return values * lax.rsqrt(mean_square + 1e-06) * scale_gain


def ring_order(n):
    if n % 2:
        return list(range(n))
    return list(range(0, n, 2)) + list(range(n - 1, 0, -2))


def ring_reduce_scatter(blocks, ring, pos):
    n, rows, _ = blocks.shape
    half = rows // 2
    ring_index = jnp.array(ring, dtype=jnp.int32)
    forward = [(ring[q], ring[(q + 1) % n]) for q in range(n)]
    backward = [(ring[q], ring[(q - 1) % n]) for q in range(n)]
    got_fwd = got_bwd = None
    for step in range(n - 1):
        owner_fwd = ring_index[(pos - 1 - step) % n]
        owner_bwd = ring_index[(pos + 1 + step) % n]
        send_fwd = lax.dynamic_index_in_dim(blocks, owner_fwd, 0, keepdims=False)[:half]
        send_bwd = lax.dynamic_index_in_dim(blocks, owner_bwd, 0, keepdims=False)[half:]
        if step:
            send_fwd = send_fwd + got_fwd
            send_bwd = send_bwd + got_bwd
        send_fwd, send_bwd = lax.optimization_barrier(
            (send_fwd.astype(jnp.bfloat16), send_bwd.astype(jnp.bfloat16))
        )
        got_fwd, got_bwd = lax.optimization_barrier(
            (lax.ppermute(send_fwd, "ep", forward), lax.ppermute(send_bwd, "ep", backward))
        )
        got_fwd = got_fwd.astype(jnp.float32)
        got_bwd = got_bwd.astype(jnp.float32)
    me = ring_index[pos]
    own = lax.dynamic_index_in_dim(blocks, me, 0, keepdims=False)
    return jnp.concatenate([own[:half] + got_fwd, own[half:] + got_bwd], axis=0)


def ring_all_gather(block, ring, pos):
    n = len(ring)
    half = block.shape[0] // 2
    forward = [(ring[q], ring[(q + 1) % n]) for q in range(n)]
    backward = [(ring[q], ring[(q - 1) % n]) for q in range(n)]
    got_fwd, got_bwd = block[:half], block[half:]
    arrived = []
    for step in range(n - 1):
        got_fwd, got_bwd = lax.optimization_barrier(
            (lax.ppermute(got_fwd, "ep", forward), lax.ppermute(got_bwd, "ep", backward))
        )
        arrived.append((got_fwd, got_bwd))
    return arrived


def ring_reduce_scatter_steps(pieces, own, ring):
    n = len(ring)
    forward = [(ring[q], ring[(q + 1) % n]) for q in range(n)]
    backward = [(ring[q], ring[(q - 1) % n]) for q in range(n)]
    got_fwd = got_bwd = None
    for step in range(n - 1):
        send_fwd, send_bwd = pieces[step]
        if step:
            send_fwd = send_fwd + got_fwd
            send_bwd = send_bwd + got_bwd
        send_fwd, send_bwd = lax.optimization_barrier(
            (send_fwd.astype(jnp.bfloat16), send_bwd.astype(jnp.bfloat16))
        )
        got_fwd, got_bwd = lax.optimization_barrier(
            (lax.ppermute(send_fwd, "ep", forward), lax.ppermute(send_bwd, "ep", backward))
        )
        got_fwd = got_fwd.astype(jnp.float32)
        got_bwd = got_bwd.astype(jnp.float32)
    half = own.shape[0] // 2
    return jnp.concatenate([own[:half] + got_fwd, own[half:] + got_bwd], axis=0)


def expert_mix(rows, weights, gate_up, down):
    hidden_width = down.shape[1]
    total = None
    for e in range(gate_up.shape[0]):
        projected_up = jnp.dot(rows, gate_up[e], preferred_element_type=jnp.float32)
        activated = (
            jax.nn.silu(projected_up[:, :hidden_width]) * projected_up[:, hidden_width:]
        ).astype(jnp.bfloat16)
        expert_out = jnp.dot(activated, down[e], preferred_element_type=jnp.float32).astype(
            jnp.bfloat16
        )
        term = weights[:, e : e + 1] * expert_out.astype(jnp.float32)
        total = term if total is None else total + term
    return total


def body(
    residual, attn_out, out_weight, post_gain, gate_up, down, route_ids, route_weight, final_gain
):
    row_count, model_width = residual.shape
    ep_size = lax.axis_size("ep")
    me = lax.axis_index("ep")
    local_experts = gate_up.shape[0]
    hidden_width = down.shape[1]
    slice_width = out_weight.shape[0]
    group_rows = row_count * ep_size
    ring = ring_order(ep_size)
    pos = jnp.array([ring.index(p) for p in range(ep_size)], dtype=jnp.int32)[me]

    with jax.named_scope("route_weights"):
        expert_ids = jnp.arange(local_experts * ep_size, dtype=jnp.int32)
        dense_weight = jnp.sum(
            jnp.where(route_ids[:, :, None] == expert_ids, route_weight[:, :, None], 0.0), axis=1
        )
        dense_weight = dense_weight.reshape(row_count, ep_size, local_experts).transpose(1, 0, 2)
        row_weights = lax.all_to_all(dense_weight, "ep", split_axis=0, concat_axis=0, tiled=True)
        row_weights = row_weights.reshape(group_rows, local_experts)

    with jax.named_scope("out_projection"):
        columns = attn_out.reshape(row_count, ep_size, slice_width).transpose(1, 0, 2)
        columns = lax.all_to_all(columns, "ep", split_axis=0, concat_axis=0, tiled=True)
        columns, row_weights = lax.optimization_barrier((columns, row_weights))
        partial = jnp.dot(
            columns.reshape(group_rows, slice_width), out_weight, preferred_element_type=jnp.float32
        )
        projected = ring_reduce_scatter(partial.reshape(ep_size, row_count, model_width), ring, pos)
        middle = (residual.astype(jnp.float32) + projected).astype(jnp.bfloat16)

    normed = rms_scale(middle.astype(jnp.float32), post_gain).astype(jnp.bfloat16)
    with jax.named_scope("dispatch_gather"):
        arrived = ring_all_gather(normed, ring, pos)

    ring_index = jnp.array(ring, dtype=jnp.int32)
    weight_blocks = row_weights.reshape(ep_size, row_count, local_experts)
    half = row_count // 2

    def step_weights(step):
        owner_fwd = ring_index[(pos - 1 - step) % ep_size]
        owner_bwd = ring_index[(pos + 1 + step) % ep_size]
        w_fwd = lax.dynamic_index_in_dim(weight_blocks, owner_fwd, 0, keepdims=False)[:half]
        w_bwd = lax.dynamic_index_in_dim(weight_blocks, owner_bwd, 0, keepdims=False)[half:]
        return w_fwd, w_bwd

    with jax.named_scope("local_experts"):
        steps_all = list(range(ep_size - 1))
        chunks = [steps_all[i : i + 2] for i in range(0, ep_size - 1, 2)]
        pieces = [None] * (ep_size - 1)
        own_part = None
        for c, steps in enumerate(chunks):
            rows_in = []
            weights_in = []
            for step in steps:
                rows_in += list(arrived[step])
                weights_in += list(step_weights(step))
            if c == 0:
                rows_in.append(normed)
                weights_in.append(lax.dynamic_index_in_dim(weight_blocks, me, 0, keepdims=False))
            mixed = expert_mix(
                jnp.concatenate(rows_in, axis=0), jnp.concatenate(weights_in, axis=0), gate_up, down
            )
            for i, step in enumerate(steps):
                pieces[step] = (mixed[(2 * i) * half : (2 * i + 1) * half],
                                mixed[(2 * i + 1) * half : (2 * i + 2) * half])
            if c == 0:
                own_part = mixed[2 * len(steps) * half :]

    with jax.named_scope("combine_return"):
        combined = ring_reduce_scatter_steps(pieces, own_part, ring)
    updated = middle.astype(jnp.float32) + combined
    return (updated.astype(jnp.bfloat16), rms_scale(updated, final_gain).astype(jnp.bfloat16))


def solution(mesh):
    in_specs = (
        P(("rep", "ep"), None),
        P(("rep", "ep"), None),
        P("ep", None),
        P(),
        P("ep", None, None),
        P("ep", None, None),
        P(("rep", "ep"), None),
        P(("rep", "ep"), None),
        P(),
    )
    out_specs = (P(("rep", "ep"), None), P(("rep", "ep"), None))
    return jax.shard_map(body, mesh=mesh, in_specs=in_specs, out_specs=out_specs, check_vma=False)
```

```python
import jax
import jax.numpy as jnp
from jax import lax
from jax.sharding import PartitionSpec as P


def rms_scale(values, scale_gain):
    mean_square = jnp.mean(values * values, axis=-1, keepdims=True)
    return values * lax.rsqrt(mean_square + 1e-06) * scale_gain


def ring_order(n):
    if n % 2:
        return list(range(n))
    return list(range(0, n, 2)) + list(range(n - 1, 0, -2))


def ring_reduce_scatter(blocks, ring, pos):
    n, rows, _ = blocks.shape
    half = rows // 2
    ring_index = jnp.array(ring, dtype=jnp.int32)
    forward = [(ring[q], ring[(q + 1) % n]) for q in range(n)]
    backward = [(ring[q], ring[(q - 1) % n]) for q in range(n)]
    got_fwd = got_bwd = None
    for step in range(n - 1):
        owner_fwd = ring_index[(pos - 1 - step) % n]
        owner_bwd = ring_index[(pos + 1 + step) % n]
        send_fwd = lax.dynamic_index_in_dim(blocks, owner_fwd, 0, keepdims=False)[:half]
        send_bwd = lax.dynamic_index_in_dim(blocks, owner_bwd, 0, keepdims=False)[half:]
        if step:
            send_fwd = send_fwd + got_fwd
            send_bwd = send_bwd + got_bwd
        send_fwd, send_bwd = lax.optimization_barrier(
            (send_fwd.astype(jnp.bfloat16), send_bwd.astype(jnp.bfloat16))
        )
        got_fwd, got_bwd = lax.optimization_barrier(
            (lax.ppermute(send_fwd, "ep", forward), lax.ppermute(send_bwd, "ep", backward))
        )
        got_fwd = got_fwd.astype(jnp.float32)
        got_bwd = got_bwd.astype(jnp.float32)
    me = ring_index[pos]
    own = lax.dynamic_index_in_dim(blocks, me, 0, keepdims=False)
    return jnp.concatenate([own[:half] + got_fwd, own[half:] + got_bwd], axis=0)


def ring_all_gather(block, ring, pos):
    n = len(ring)
    half = block.shape[0] // 2
    forward = [(ring[q], ring[(q + 1) % n]) for q in range(n)]
    backward = [(ring[q], ring[(q - 1) % n]) for q in range(n)]
    got_fwd, got_bwd = block[:half], block[half:]
    arrived = []
    for step in range(n - 1):
        got_fwd, got_bwd = lax.optimization_barrier(
            (lax.ppermute(got_fwd, "ep", forward), lax.ppermute(got_bwd, "ep", backward))
        )
        arrived.append((got_fwd, got_bwd))
    return arrived


def ring_reduce_scatter_steps(pieces, own, ring):
    n = len(ring)
    forward = [(ring[q], ring[(q + 1) % n]) for q in range(n)]
    backward = [(ring[q], ring[(q - 1) % n]) for q in range(n)]
    got_fwd = got_bwd = None
    for step in range(n - 1):
        send_fwd, send_bwd = pieces[step]
        if step:
            send_fwd = send_fwd + got_fwd
            send_bwd = send_bwd + got_bwd
        send_fwd, send_bwd = lax.optimization_barrier(
            (send_fwd.astype(jnp.bfloat16), send_bwd.astype(jnp.bfloat16))
        )
        got_fwd, got_bwd = lax.optimization_barrier(
            (lax.ppermute(send_fwd, "ep", forward), lax.ppermute(send_bwd, "ep", backward))
        )
        got_fwd = got_fwd.astype(jnp.float32)
        got_bwd = got_bwd.astype(jnp.float32)
    half = own.shape[0] // 2
    return jnp.concatenate([own[:half] + got_fwd, own[half:] + got_bwd], axis=0)


def expert_mix(rows, weights, gate_up, down):
    hidden_width = down.shape[1]
    total = None
    for e in range(gate_up.shape[0]):
        projected_up = jnp.dot(rows, gate_up[e], preferred_element_type=jnp.float32)
        activated = (
            jax.nn.silu(projected_up[:, :hidden_width]) * projected_up[:, hidden_width:]
        ).astype(jnp.bfloat16)
        expert_out = jnp.dot(activated, down[e], preferred_element_type=jnp.float32).astype(
            jnp.bfloat16
        )
        term = weights[:, e : e + 1] * expert_out.astype(jnp.float32)
        total = term if total is None else total + term
    return total


def body(
    residual, attn_out, out_weight, post_gain, gate_up, down, route_ids, route_weight, final_gain
):
    row_count, model_width = residual.shape
    ep_size = lax.axis_size("ep")
    me = lax.axis_index("ep")
    local_experts = gate_up.shape[0]
    hidden_width = down.shape[1]
    slice_width = out_weight.shape[0]
    group_rows = row_count * ep_size
    ring = ring_order(ep_size)
    pos = jnp.array([ring.index(p) for p in range(ep_size)], dtype=jnp.int32)[me]

    with jax.named_scope("route_weights"):
        expert_ids = jnp.arange(local_experts * ep_size, dtype=jnp.int32)
        dense_weight = jnp.sum(
            jnp.where(route_ids[:, :, None] == expert_ids, route_weight[:, :, None], 0.0), axis=1
        )
        dense_weight = dense_weight.reshape(row_count, ep_size, local_experts).transpose(1, 0, 2)
        row_weights = lax.all_to_all(dense_weight, "ep", split_axis=0, concat_axis=0, tiled=True)
        row_weights = row_weights.reshape(group_rows, local_experts)

    with jax.named_scope("out_projection"):
        columns = attn_out.reshape(row_count, ep_size, slice_width).transpose(1, 0, 2)
        columns = lax.all_to_all(columns, "ep", split_axis=0, concat_axis=0, tiled=True)
        columns, row_weights = lax.optimization_barrier((columns, row_weights))
        partial = jnp.dot(
            columns.reshape(group_rows, slice_width), out_weight, preferred_element_type=jnp.float32
        )
        projected = ring_reduce_scatter(partial.reshape(ep_size, row_count, model_width), ring, pos)
        middle = (residual.astype(jnp.float32) + projected).astype(jnp.bfloat16)

    normed = rms_scale(middle.astype(jnp.float32), post_gain).astype(jnp.bfloat16)
    with jax.named_scope("dispatch_gather"):
        arrived = ring_all_gather(normed, ring, pos)

    ring_index = jnp.array(ring, dtype=jnp.int32)
    weight_blocks = row_weights.reshape(ep_size, row_count, local_experts)
    half = row_count // 2

    def step_weights(step):
        owner_fwd = ring_index[(pos - 1 - step) % ep_size]
        owner_bwd = ring_index[(pos + 1 + step) % ep_size]
        w_fwd = lax.dynamic_index_in_dim(weight_blocks, owner_fwd, 0, keepdims=False)[:half]
        w_bwd = lax.dynamic_index_in_dim(weight_blocks, owner_bwd, 0, keepdims=False)[half:]
        return w_fwd, w_bwd

    with jax.named_scope("local_experts"):
        steps_all = list(range(ep_size - 1))
        chunks = [steps_all[i : i + 2] for i in range(0, ep_size - 1, 2)]
        pieces = [None] * (ep_size - 1)
        own_part = None
        for c, steps in enumerate(chunks):
            rows_in = []
            weights_in = []
            for step in steps:
                rows_in += list(arrived[step])
                weights_in += list(step_weights(step))
            if c == 1:
                rows_in.append(normed)
                weights_in.append(lax.dynamic_index_in_dim(weight_blocks, me, 0, keepdims=False))
            mixed = expert_mix(
                jnp.concatenate(rows_in, axis=0), jnp.concatenate(weights_in, axis=0), gate_up, down
            )
            for i, step in enumerate(steps):
                pieces[step] = (mixed[(2 * i) * half : (2 * i + 1) * half],
                                mixed[(2 * i + 1) * half : (2 * i + 2) * half])
            if c == 1:
                own_part = mixed[2 * len(steps) * half :]

    with jax.named_scope("combine_return"):
        combined = ring_reduce_scatter_steps(pieces, own_part, ring)
    updated = middle.astype(jnp.float32) + combined
    return (updated.astype(jnp.bfloat16), rms_scale(updated, final_gain).astype(jnp.bfloat16))


def solution(mesh):
    in_specs = (
        P(("rep", "ep"), None),
        P(("rep", "ep"), None),
        P("ep", None),
        P(),
        P("ep", None, None),
        P("ep", None, None),
        P(("rep", "ep"), None),
        P(("rep", "ep"), None),
        P(),
    )
    out_specs = (P(("rep", "ep"), None), P(("rep", "ep"), None))
    return jax.shard_map(body, mesh=mesh, in_specs=in_specs, out_specs=out_specs, check_vma=False)
```
